256 devices in a mesh: row: 32 (over x, y, core), col: 8 (over z).
Axes of the slice: x: 4, y: 4, z: 8, core: 2. Of those that a mesh axis runs over, the one named last changes fastest.
Arguments:
- leaf_points: float32 [128, 8, 256], P('row'), may hold values from -6 to 6
- col_points: float32 [8, 512, 8, 256], P('col', 'row'), may hold values from -6 to 6
- source_hash_signs: int32 [8, 512, 256], P('col'), may hold values from 0 to 255
- adjacent_leaf_lists: int32 [128, 384], P('row', 'col'), may hold values from 0 to 511
- near_count: int32 [128, 8], P('row', 'col'), may hold values from 1 to 48, as said below
Outputs:
- leaf_basis: float32 [128, 256, 128], P('row', 'col')
- top_factor: float32 [32, 128, 128], P('row')
The draws below stay inside these ranges and needn't reach their ends.
Inputs may be any that keep to these rules, and one draw needn't show every extreme that they name: `adjacent_leaf_lists`: A column leaf number local to owner c; slots at or beyond the pair's count are unused. `near_count`: some pair has exactly 48 used slots. `source_hash_signs`: the bucket is code % 128, the sign is negative where code >= 128.
All inputs are finite; a program needn't handle non-finite values.
Results may differ from the reference program's by a relative error of at most 0.0003.
Values sent between devices are 32-bit elements; how exact they have to be, the bound alone decides.
No kernel may reach another device: no remote copies, remote signals or barrier semaphores. Data moves between devices by JAX's collectives and lax.ppermute only.
A program may use at most 64 MiB of HBM per device.

```python
from functools import partial
import jax
import jax.numpy as jnp
from jax import lax

DIM = 8
LEAF = 256
SK = 128
MERGED_LEVELS = 4
LEAF_DEV = 4
NEAR = 48
NLEAF = 128
NOWN = 512
N_ROW = 32
N_COL = 8


def draw_near_count(key, part):
    key_weight = jax.random.fold_in(key, 11)
    random_key_seed = jax.random.fold_in(key, 12)
    key_pick = jax.random.fold_in(key, 13)
    sample_weight = jnp.left_shift(jnp.ones((N_COL,), jnp.int32), jax.random.randint(key_weight, (N_COL,), 0, 4).astype(jnp.int32))
    base = jax.random.randint(random_key_seed, (NLEAF, N_COL), 0, NEAR).astype(jnp.int32)
    counts = jnp.minimum(NEAR, 1 + base * sample_weight[None, :] // 8).reshape(-1)
    pick = jax.random.randint(key_pick, (), 0, NLEAF * N_COL).astype(jnp.int32)
    counts = jnp.where(jnp.arange(NLEAF * N_COL, dtype=jnp.int32) == pick, NEAR, counts)
    return counts.reshape(NLEAF, N_COL).astype(jnp.int32)


def touch_ends(values, own_key, low, top_value):
    longest = values.shape.index(max(values.shape))
    spots = []
    for shift in (0, 1):
        where = [jax.random.randint(jax.random.fold_in(own_key, axis), (), 0, length) for axis, length in enumerate(values.shape)]
        where[longest] = (where[longest] + shift) % values.shape[longest]
        spots.append(tuple(where))
    return values.at[spots[0]].set(low).at[spots[1]].set(top_value)


def block_scale(stream_key, shape, pieces, least, largest):
    def one(position, blocks):
        heights = jax.random.uniform(jax.random.fold_in(jax.random.fold_in(stream_key, 6), position), (blocks,), jnp.float32, least / len(pieces), largest / len(pieces))
        return jnp.repeat(jnp.exp(heights), shape[position] // blocks).reshape((-1,) + (1,) * (len(shape) - position - 1))

    gain = one(*pieces[0])
    for cut in pieces[1:]:
        gain = gain * one(*cut)
    return gain


def bell_draw(stream_key, shape, width, limit, pieces=(), kind=jnp.bfloat16):
    drawn = width * jax.random.normal(stream_key, shape, jnp.float32)
    if pieces:
        drawn = drawn * block_scale(stream_key, shape, pieces, -0.22, 0.18)
    return jnp.clip(drawn, -limit, limit).astype(kind)


def setup_inputs(seed: int = 0) -> dict:
    key_list = jax.random.split(jax.random.key(seed), 6)
    return {
        "leaf_points": bell_draw(key_list[0], (NLEAF, DIM, LEAF), 1.0, 6.0, ((0, 32),), jnp.float32),
        "col_points": bell_draw(key_list[1], (N_COL, NOWN, DIM, LEAF), 1.0, 6.0, ((0, 8), (1, 32)), jnp.float32),
        "source_hash_signs": touch_ends(jax.random.randint(key_list[2], (N_COL, NOWN, LEAF), 0, 2 * SK), jax.random.fold_in(key_list[2], 1), 0, (2 * SK) - 1).astype(jnp.int32),
        "adjacent_leaf_lists": touch_ends(jax.random.randint(key_list[3], (NLEAF, N_COL * NEAR), 0, NOWN), jax.random.fold_in(key_list[3], 1), 0, NOWN - 1).astype(jnp.int32),
        "near_count": draw_near_count(jax.random.fold_in(key_list[5], 71), 0),
    }


half_inverse = 0.125
ridge_eps = 1e-05

def tile_samples(output_kernel_patch, source_kernel_patch, code_block, live):
    inner_dots_matrix = jnp.einsum('qjn,qjp->qnp', output_kernel_patch, source_kernel_patch, precision=lax.Precision.HIGHEST)
    output_squared_norms = jnp.sum(output_kernel_patch * output_kernel_patch, axis=1)
    col_sq = jnp.sum(source_kernel_patch * source_kernel_patch, axis=1)
    kernel = jnp.exp(-(output_squared_norms[:, :, None] + col_sq[:, None, :] - 2.0 * inner_dots_matrix) * half_inverse) * live[:, None, None]
    bucket = code_block % SK
    signs = (1 - 2 * (code_block // SK)).astype(jnp.float32)
    omega = jnp.where(bucket[:, :, None] == jnp.arange(SK, dtype=jnp.int32)[None, None, :], signs[:, :, None], 0.0).astype(jnp.float32)
    return jnp.einsum('bij,bjk->bik', kernel, omega, precision=lax.Precision.HIGHEST)

def merge_pair(first_child, second_child):
    gram = jnp.einsum('bji,bjk->bik', first_child, first_child, precision=lax.Precision.HIGHEST)
    gram = gram + jnp.einsum('bji,bjk->bik', second_child, second_child, precision=lax.Precision.HIGHEST)
    return jnp.swapaxes(jnp.linalg.cholesky(gram), 1, 2)

def reference(leaf_points, col_points, source_hash_signs, adjacent_leaf_lists, near_count):
    slot_table = adjacent_leaf_lists.reshape(NLEAF, N_COL, NEAR)

    def one_leaf(stacked_entries):
        row_points, slots, counts = stacked_entries

        def per_owner(total, owner):
            column = slots[owner]
            source_kernel_patch = col_points[owner][column]
            code_block = source_hash_signs[owner][column]
            live = (jnp.arange(NEAR, dtype=jnp.int32) < counts[owner]).astype(jnp.float32)
            output_kernel_patch = jnp.broadcast_to(row_points[None], source_kernel_patch.shape)
            terms = tile_samples(output_kernel_patch, source_kernel_patch, code_block, live)
            return (total + jnp.sum(terms, axis=0), None)
        start = jnp.zeros((LEAF, SK), jnp.float32)
        total, unused = lax.scan(per_owner, start, jnp.arange(N_COL, dtype=jnp.int32))
        return total
    samples = lax.map(one_leaf, (leaf_points, slot_table, near_count))
    gram = jnp.einsum('bri,brk->bik', samples, samples, precision=lax.Precision.HIGHEST)
    ridge = jnp.trace(gram, axis1=1, axis2=2) / SK + ridge_eps
    lower = jnp.linalg.cholesky(gram + ridge[:, None, None] * jnp.eye(SK, dtype=jnp.float32)[None])
    triangular_backsubstitute = jax.vmap(partial(jax.scipy.linalg.solve_triangular, lower=True))
    leaf_basis = jnp.swapaxes(triangular_backsubstitute(lower, jnp.swapaxes(samples, 1, 2)), 1, 2)
    factor = jnp.swapaxes(lower, 1, 2)
    for level in range(MERGED_LEVELS):
        pairs = factor.reshape(-1, 2, SK, SK)
        factor = merge_pair(pairs[:, 0], pairs[:, 1])
    which = jnp.arange(N_ROW, dtype=jnp.int32) * LEAF_DEV // 2 ** MERGED_LEVELS
    return (leaf_basis, factor[which])
```

```python
from functools import partial

import jax
import jax.numpy as jnp
from jax import lax
from jax.sharding import PartitionSpec as P

SK = 128
MERGED_LEVELS = 4


half_inverse = 0.125
ridge_eps = 1e-05
block_tiles = 16


def from_partner(value, axis, stride):
    mask = 2**stride
    pairs = [(source, source ^ mask) for source in range(lax.axis_size(axis))]
    return lax.ppermute(value, axis, pairs)


def tile_samples(output_kernel_patch, source_kernel_patch, code_block, live):
    inner_dots_matrix = jnp.einsum(
        "qjn,qjp->qnp", output_kernel_patch, source_kernel_patch, precision=lax.Precision.HIGHEST
    )
    output_squared_norms = jnp.sum(output_kernel_patch * output_kernel_patch, axis=1)
    col_sq = jnp.sum(source_kernel_patch * source_kernel_patch, axis=1)
    kernel = (
        jnp.exp(
            -(output_squared_norms[:, :, None] + col_sq[:, None, :] - 2.0 * inner_dots_matrix)
            * half_inverse
        )
        * live[:, None, None]
    )
    bucket = code_block % SK
    signs = (1 - 2 * (code_block // SK)).astype(jnp.float32)
    omega = jnp.where(
        bucket[:, :, None] == jnp.arange(SK, dtype=jnp.int32)[None, None, :], signs[:, :, None], 0.0
    )
    return jnp.einsum("bij,bjk->bik", kernel, omega, precision=lax.Precision.HIGHEST)


def merge_pair(first_child, second_child):
    gram = jnp.einsum("bji,bjk->bik", first_child, first_child, precision=lax.Precision.HIGHEST)
    gram = gram + jnp.einsum(
        "bji,bjk->bik", second_child, second_child, precision=lax.Precision.HIGHEST
    )
    return jnp.swapaxes(jnp.linalg.cholesky(gram), 1, 2)


def accumulate(
    row_points, col_store, code_store, slot_table, pair_count, pair_leaf, pair_owner, last
):
    bounds = jnp.cumsum(pair_count)
    leaves = row_points.shape[0]

    def advance(turn, samples):
        ranks = turn * block_tiles + jnp.arange(block_tiles, dtype=jnp.int32)
        live = ranks < last
        ranks = jnp.minimum(ranks, last - 1)
        pair = jnp.sum((bounds[None, :] <= ranks[:, None]).astype(jnp.int32), axis=1)
        slot = ranks - (bounds[pair] - pair_count[pair])
        column = slot_table[pair, slot]
        owner = pair_owner[pair]
        target = pair_leaf[pair]
        source_kernel_patch = col_store[owner, column]
        code_block = code_store[owner, column]
        output_kernel_patch = row_points[target]
        terms = tile_samples(
            output_kernel_patch, source_kernel_patch, code_block, live.astype(jnp.float32)
        )
        selected_rows = (
            (target[:, None] == jnp.arange(leaves, dtype=jnp.int32)[None, :]) & live[:, None]
        ).astype(jnp.float32)
        return samples + jnp.einsum(
            "bl,bik->lik", selected_rows, terms, precision=lax.Precision.HIGHEST
        )

    turns = (last + block_tiles - 1) // block_tiles
    start = jnp.zeros((leaves, row_points.shape[2], SK), jnp.float32)
    return lax.fori_loop(0, turns, advance, start)


def on_device(leaf_points, col_points, source_hash_signs, adjacent_leaf_lists, near_count):
    owned = lax.all_gather(col_points, "row", axis=1, tiled=True)
    leaves = leaf_points.shape[0]
    pair_count = near_count[:, 0]
    samples = accumulate(
        leaf_points,
        owned,
        source_hash_signs,
        adjacent_leaf_lists,
        pair_count,
        jnp.arange(leaves, dtype=jnp.int32),
        jnp.zeros((leaves,), jnp.int32),
        jnp.sum(pair_count),
    )
    samples = lax.psum(samples, "col")
    rows = samples.shape[1] // lax.axis_size("col")
    rows_part = lax.dynamic_slice_in_dim(samples, lax.axis_index("col") * rows, rows, axis=1)
    gram = jnp.einsum("bri,brk->bik", samples, samples, precision=lax.Precision.HIGHEST)
    ridge = jnp.trace(gram, axis1=1, axis2=2) / SK + ridge_eps
    shifted = gram + ridge[:, None, None] * jnp.eye(SK, dtype=jnp.float32)[None]
    lower = jnp.linalg.cholesky(shifted)
    triangular_backsubstitute = jax.vmap(partial(jax.scipy.linalg.solve_triangular, lower=True))
    leaf_basis = jnp.swapaxes(triangular_backsubstitute(lower, jnp.swapaxes(rows_part, 1, 2)), 1, 2)
    total = jnp.sum(shifted, axis=0)
    local_levels = leaves.bit_length() - 1
    for bit in range(MERGED_LEVELS - local_levels):
        total = total + from_partner(total, "row", bit)
    factor = jnp.swapaxes(jnp.linalg.cholesky(total[None]), 1, 2)
    return (leaf_basis, factor)


def solution(mesh):
    return jax.shard_map(
        on_device,
        mesh=mesh,
        in_specs=(
            P("row", None, None),
            P("col", "row", None, None),
            P("col", None, None),
            P("row", "col"),
            P("row", "col"),
        ),
        out_specs=(P("row", "col", None), P("row", None, None)),
        check_vma=False,
    )
```

```python
from functools import partial

import jax
import jax.numpy as jnp
from jax import lax
from jax.sharding import PartitionSpec as P
from jax.experimental import pallas as pl
from jax.experimental.pallas import tpu as pltpu

SK = 128
MERGED_LEVELS = 4


half_inverse = 0.125
ridge_eps = 1e-05


def from_partner(value, axis, stride):
    mask = 2**stride
    pairs = [(source, source ^ mask) for source in range(lax.axis_size(axis))]
    return lax.ppermute(value, axis, pairs)


def split3(value):
    first = value.astype(jnp.bfloat16)
    rest = value - first.astype(jnp.float32)
    second = rest.astype(jnp.bfloat16)
    third = (rest - second.astype(jnp.float32)).astype(jnp.bfloat16)
    return first, second, third


def row_operand(leaf_points):
    norms = jnp.sum(leaf_points * leaf_points, axis=1)
    scaled = jnp.swapaxes(leaf_points, 1, 2) * (2.0 * half_inverse)
    place = lax.broadcasted_iota(jnp.int32, norms.shape + (8,), 2)
    tail = jnp.where(place == 0, -half_inverse, jnp.where(place == 1, -half_inverse * norms[:, :, None], 0.0))
    first, second, third = split3(jnp.concatenate([scaled, tail], axis=2))
    return jnp.concatenate([first, first, second, second, first, third], axis=2)


def sketch_kernel(slots_ref, counts_ref, row_ref, col_ref, code_ref, out_ref):
    leaves = out_ref.shape[0]
    points = col_ref.shape[2]
    place = lax.broadcasted_iota(jnp.int32, (8, points), 0)
    bucket_id = lax.broadcasted_iota(jnp.int32, (SK, points), 0)
    contract_last = (((1,), (1,)), ((), ()))
    for leaf in range(leaves):
        out_ref[leaf] = jnp.zeros(out_ref.shape[1:], jnp.float32)

        def tile(slot, carry):
            column = slots_ref[leaf, slot]
            y = col_ref[column]
            norms = jnp.sum(y * y, axis=0, keepdims=True)
            tail = jnp.where(place == 0, norms, jnp.where(place == 1, 1.0, 0.0))
            first, second, third = split3(jnp.concatenate([y, tail], axis=0))
            stacked = jnp.concatenate([first, second, first, second, third, first], axis=0)
            exponent = jnp.dot(row_ref[leaf], stacked, preferred_element_type=jnp.float32)
            kernel = jnp.exp(exponent)
            code = code_ref[pl.ds(column, 1), :]
            signs = (1 - 2 * (code // SK)).astype(jnp.float32)
            omega_t = jnp.where(bucket_id == code % SK, signs, 0.0).astype(jnp.bfloat16)
            high = kernel.astype(jnp.bfloat16)
            low = (kernel - high.astype(jnp.float32)).astype(jnp.bfloat16)
            terms = lax.dot_general(high, omega_t, contract_last, preferred_element_type=jnp.float32)
            terms = terms + lax.dot_general(low, omega_t, contract_last, preferred_element_type=jnp.float32)
            out_ref[leaf] += terms
            return carry

        def two_tiles(step, carry):
            return tile(2 * step + 1, tile(2 * step, carry))

        count = counts_ref[leaf]
        lax.fori_loop(0, count // 2, two_tiles, 0)
        lax.fori_loop((count // 2) * 2, count, tile, 0)


def accumulate(leaf_points, col_store, code_store, slot_table, pair_count):
    leaves, _, points = leaf_points.shape
    smem, vmem = pltpu.MemorySpace.SMEM, pltpu.MemorySpace.VMEM
    return pl.pallas_call(
        sketch_kernel,
        out_shape=jax.ShapeDtypeStruct((leaves, points, SK), jnp.float32),
        in_specs=[pl.BlockSpec(memory_space=smem)] * 2 + [pl.BlockSpec(memory_space=vmem)] * 3,
        out_specs=pl.BlockSpec(memory_space=vmem),
        compiler_params=pltpu.CompilerParams(vmem_limit_bytes=48 * 1024 * 1024),
    )(slot_table, pair_count, row_operand(leaf_points), col_store, code_store)


def on_device(leaf_points, col_points, source_hash_signs, adjacent_leaf_lists, near_count):
    owned = lax.all_gather(col_points, "row", axis=1, tiled=True)
    leaves = leaf_points.shape[0]
    pair_count = near_count[:, 0]
    samples = accumulate(
        leaf_points,
        owned.reshape(owned.shape[1:]),
        source_hash_signs.reshape(source_hash_signs.shape[1:]),
        adjacent_leaf_lists,
        pair_count,
    )
    samples = lax.psum(samples, "col")
    rows = samples.shape[1] // lax.axis_size("col")
    rows_part = lax.dynamic_slice_in_dim(samples, lax.axis_index("col") * rows, rows, axis=1)
    gram = jnp.einsum("bri,brk->bik", samples, samples, precision=lax.Precision.HIGHEST)
    ridge = jnp.trace(gram, axis1=1, axis2=2) / SK + ridge_eps
    shifted = gram + ridge[:, None, None] * jnp.eye(SK, dtype=jnp.float32)[None]
    lower = jnp.linalg.cholesky(shifted)
    triangular_backsubstitute = jax.vmap(partial(jax.scipy.linalg.solve_triangular, lower=True))
    leaf_basis = jnp.swapaxes(triangular_backsubstitute(lower, jnp.swapaxes(rows_part, 1, 2)), 1, 2)
    total = jnp.sum(shifted, axis=0)
    local_levels = leaves.bit_length() - 1
    for bit in range(MERGED_LEVELS - local_levels):
        total = total + from_partner(total, "row", bit)
    factor = jnp.swapaxes(jnp.linalg.cholesky(total[None]), 1, 2)
    return (leaf_basis, factor)


def solution(mesh):
    return jax.shard_map(
        on_device,
        mesh=mesh,
        in_specs=(
            P("row", None, None),
            P("col", "row", None, None),
            P("col", None, None),
            P("row", "col"),
            P("row", "col"),
        ),
        out_specs=(P("row", "col", None), P("row", None, None)),
        check_vma=False,
    )
```

```python
from functools import partial

import jax
import jax.numpy as jnp
from jax import lax
from jax.sharding import PartitionSpec as P
from jax.experimental import pallas as pl
from jax.experimental.pallas import tpu as pltpu

SK = 128
MERGED_LEVELS = 4


half_inverse = 0.125
ridge_eps = 1e-05


def from_partner(value, axis, stride):
    mask = 2**stride
    pairs = [(source, source ^ mask) for source in range(lax.axis_size(axis))]
    return lax.ppermute(value, axis, pairs)


def split3(value):
    first = value.astype(jnp.bfloat16)
    rest = value - first.astype(jnp.float32)
    second = rest.astype(jnp.bfloat16)
    third = (rest - second.astype(jnp.float32)).astype(jnp.bfloat16)
    return first, second, third


def row_operand(leaf_points):
    norms = jnp.sum(leaf_points * leaf_points, axis=1)
    scaled = jnp.swapaxes(leaf_points, 1, 2) * (2.0 * half_inverse)
    place = lax.broadcasted_iota(jnp.int32, norms.shape + (8,), 2)
    tail = jnp.where(place == 0, -half_inverse, jnp.where(place == 1, -half_inverse * norms[:, :, None], 0.0))
    first, second, third = split3(jnp.concatenate([scaled, tail], axis=2))
    return jnp.concatenate([first, first, second, second, first, third], axis=2)


def sketch_kernel(slots_ref, counts_ref, row_ref, col_ref, code_ref, out_ref):
    leaves = out_ref.shape[0]
    points = col_ref.shape[2]
    place = lax.broadcasted_iota(jnp.int32, (8, points), 0)
    bucket_id = lax.broadcasted_iota(jnp.int32, (SK, points), 0)
    contract_last = (((1,), (1,)), ((), ()))
    for leaf in range(leaves):
        out_ref[leaf] = jnp.zeros(out_ref.shape[1:], jnp.float32)

        def tile(slot, carry):
            column = slots_ref[leaf, slot]
            y = col_ref[column]
            norms = jnp.sum(y * y, axis=0, keepdims=True)
            tail = jnp.where(place == 0, norms, jnp.where(place == 1, 1.0, 0.0))
            first, second, third = split3(jnp.concatenate([y, tail], axis=0))
            stacked = jnp.concatenate([first, second, first, second, third, first], axis=0)
            exponent = jnp.dot(row_ref[leaf], stacked, preferred_element_type=jnp.float32)
            kernel = jnp.exp(exponent)
            code = code_ref[pl.ds(column, 1), :]
            signs = (1 - 2 * (code // SK)).astype(jnp.float32)
            omega_t = jnp.where(bucket_id == code % SK, signs, 0.0).astype(jnp.bfloat16)
            high = kernel.astype(jnp.bfloat16)
            low = (kernel - high.astype(jnp.float32)).astype(jnp.bfloat16)
            terms = lax.dot_general(high, omega_t, contract_last, preferred_element_type=jnp.float32)
            terms = terms + lax.dot_general(low, omega_t, contract_last, preferred_element_type=jnp.float32)
            out_ref[leaf] += terms
            return carry

        def two_tiles(step, carry):
            return tile(2 * step + 1, tile(2 * step, carry))

        count = counts_ref[leaf]
        lax.fori_loop(0, count // 2, two_tiles, 0)
        lax.fori_loop((count // 2) * 2, count, tile, 0)


def accumulate(leaf_points, col_store, code_store, slot_table, pair_count):
    leaves, _, points = leaf_points.shape
    smem, vmem = pltpu.MemorySpace.SMEM, pltpu.MemorySpace.VMEM
    return pl.pallas_call(
        sketch_kernel,
        out_shape=jax.ShapeDtypeStruct((leaves, points, SK), jnp.float32),
        in_specs=[pl.BlockSpec(memory_space=smem)] * 2 + [pl.BlockSpec(memory_space=vmem)] * 3,
        out_specs=pl.BlockSpec(memory_space=vmem),
        compiler_params=pltpu.CompilerParams(vmem_limit_bytes=48 * 1024 * 1024),
    )(slot_table, pair_count, row_operand(leaf_points), col_store, code_store)


def cholesky_kernel(in_ref, out_ref):
    mats, rows, width = in_ref.shape
    out_ref[...] = in_ref[...]
    for block in range(width // 8):
        low = block * 8
        shape = (rows - low, width)
        lane = lax.broadcasted_iota(jnp.int32, shape, 1)
        row = lax.broadcasted_iota(jnp.int32, shape, 0) + low
        parts = [out_ref[m, low:, :] for m in range(mats)]
        for t in range(8):
            j = low + t
            pick = lane == j
            later = lane > j
            for m in range(mats):
                a = parts[m]
                pivot_row = a[t : t + 1]
                pivot = jnp.sum(jnp.where(pick[:1], pivot_row, 0.0), axis=1, keepdims=True)
                scale = 1.0 / jnp.sqrt(pivot)
                column = jnp.sum(jnp.where(pick, a, 0.0), axis=1, keepdims=True) * scale
                column = jnp.where(row[:, :1] >= j, column, 0.0)
                updated = a - column * (pivot_row * scale)
                parts[m] = jnp.where(later, updated, jnp.where(pick, column, a))
        for m in range(mats):
            out_ref[m, low:, :] = parts[m]
    lane = lax.broadcasted_iota(jnp.int32, (rows, width), 1)
    row = lax.broadcasted_iota(jnp.int32, (rows, width), 0)
    for m in range(mats):
        out_ref[m] = jnp.where(row >= lane, out_ref[m], 0.0)


def cholesky_rows(stacked):
    vmem = pltpu.MemorySpace.VMEM
    return pl.pallas_call(
        cholesky_kernel,
        out_shape=jax.ShapeDtypeStruct(stacked.shape, jnp.float32),
        in_specs=[pl.BlockSpec(memory_space=vmem)],
        out_specs=pl.BlockSpec(memory_space=vmem),
    )(stacked)


def on_device(leaf_points, col_points, source_hash_signs, adjacent_leaf_lists, near_count):
    owned = lax.all_gather(col_points, "row", axis=1, tiled=True)
    leaves = leaf_points.shape[0]
    pair_count = near_count[:, 0]
    samples = accumulate(
        leaf_points,
        owned.reshape(owned.shape[1:]),
        source_hash_signs.reshape(source_hash_signs.shape[1:]),
        adjacent_leaf_lists,
        pair_count,
    )
    samples = lax.psum(samples, "col")
    rows = samples.shape[1] // lax.axis_size("col")
    rows_part = lax.dynamic_slice_in_dim(samples, lax.axis_index("col") * rows, rows, axis=1)
    gram = jnp.einsum("bri,brk->bik", samples, samples, precision=lax.Precision.HIGHEST)
    ridge = jnp.trace(gram, axis1=1, axis2=2) / SK + ridge_eps
    shifted = gram + ridge[:, None, None] * jnp.eye(SK, dtype=jnp.float32)[None]
    total = jnp.sum(shifted, axis=0)
    local_levels = leaves.bit_length() - 1
    for bit in range(MERGED_LEVELS - local_levels):
        total = total + from_partner(total, "row", bit)
    stacked = jnp.concatenate(
        [
            jnp.concatenate([shifted, rows_part], axis=1),
            jnp.concatenate([total, jnp.zeros_like(rows_part[0])], axis=0)[None],
        ],
        axis=0,
    )
    factored = cholesky_rows(stacked)
    leaf_basis = factored[:leaves, SK:, :]
    factor = jnp.swapaxes(factored[leaves:, :SK, :], 1, 2)
    return (leaf_basis, factor)


def solution(mesh):
    return jax.shard_map(
        on_device,
        mesh=mesh,
        in_specs=(
            P("row", None, None),
            P("col", "row", None, None),
            P("col", None, None),
            P("row", "col"),
            P("row", "col"),
        ),
        out_specs=(P("row", "col", None), P("row", None, None)),
        check_vma=False,
    )
```

```python
from functools import partial

import jax
import jax.numpy as jnp
from jax import lax
from jax.sharding import PartitionSpec as P
from jax.experimental import pallas as pl
from jax.experimental.pallas import tpu as pltpu

SK = 128
MERGED_LEVELS = 4


half_inverse = 0.125
ridge_eps = 1e-05


def from_partner(value, axis, stride):
    mask = 2**stride
    pairs = [(source, source ^ mask) for source in range(lax.axis_size(axis))]
    return lax.ppermute(value, axis, pairs)


def split3(value):
    first = value.astype(jnp.bfloat16)
    rest = value - first.astype(jnp.float32)
    second = rest.astype(jnp.bfloat16)
    third = (rest - second.astype(jnp.float32)).astype(jnp.bfloat16)
    return first, second, third


def row_operand(leaf_points):
    norms = jnp.sum(leaf_points * leaf_points, axis=1)
    scaled = jnp.swapaxes(leaf_points, 1, 2) * (2.0 * half_inverse)
    place = lax.broadcasted_iota(jnp.int32, norms.shape + (8,), 2)
    tail = jnp.where(place == 0, -half_inverse, jnp.where(place == 1, -half_inverse * norms[:, :, None], 0.0))
    first, second, third = split3(jnp.concatenate([scaled, tail], axis=2))
    return jnp.concatenate([first, first, second, second, first, third], axis=2)


def sketch_kernel(slots_ref, counts_ref, row_ref, col_ref, code_ref, out_ref):
    leaves = out_ref.shape[0]
    points = col_ref.shape[2]
    place = lax.broadcasted_iota(jnp.int32, (8, points), 0)
    bucket_id = lax.broadcasted_iota(jnp.int32, (SK, points), 0)
    contract_last = (((1,), (1,)), ((), ()))
    for leaf in range(leaves):
        out_ref[leaf] = jnp.zeros(out_ref.shape[1:], jnp.float32)

        def tile(slot, carry):
            column = slots_ref[leaf, slot]
            y = col_ref[column]
            norms = jnp.sum(y * y, axis=0, keepdims=True)
            tail = jnp.where(place == 0, norms, jnp.where(place == 1, 1.0, 0.0))
            first, second, third = split3(jnp.concatenate([y, tail], axis=0))
            stacked = jnp.concatenate([first, second, first, second, third, first], axis=0)
            exponent = jnp.dot(row_ref[leaf], stacked, preferred_element_type=jnp.float32)
            kernel = jnp.exp(exponent)
            code = code_ref[pl.ds(column, 1), :]
            signs = (1 - 2 * (code // SK)).astype(jnp.float32)
            omega_t = jnp.where(bucket_id == code % SK, signs, 0.0).astype(jnp.bfloat16)
            high = kernel.astype(jnp.bfloat16)
            low = (kernel - high.astype(jnp.float32)).astype(jnp.bfloat16)
            terms = lax.dot_general(high, omega_t, contract_last, preferred_element_type=jnp.float32)
            terms = terms + lax.dot_general(low, omega_t, contract_last, preferred_element_type=jnp.float32)
            out_ref[leaf] += terms
            return carry

        def two_tiles(step, carry):
            return tile(2 * step + 1, tile(2 * step, carry))

        count = counts_ref[leaf]
        lax.fori_loop(0, count // 2, two_tiles, 0)
        lax.fori_loop((count // 2) * 2, count, tile, 0)


def accumulate(leaf_points, col_store, code_store, slot_table, pair_count):
    leaves, _, points = leaf_points.shape
    smem, vmem = pltpu.MemorySpace.SMEM, pltpu.MemorySpace.VMEM
    return pl.pallas_call(
        sketch_kernel,
        out_shape=jax.ShapeDtypeStruct((leaves, points, SK), jnp.float32),
        in_specs=[pl.BlockSpec(memory_space=smem)] * 2 + [pl.BlockSpec(memory_space=vmem)] * 3,
        out_specs=pl.BlockSpec(memory_space=vmem),
        compiler_params=pltpu.CompilerParams(vmem_limit_bytes=48 * 1024 * 1024),
    )(slot_table, pair_count, row_operand(leaf_points), col_store, code_store)


def cholesky_kernel(in_ref, out_ref):
    mats, rows, width = in_ref.shape
    out_ref[...] = in_ref[...]
    for block in range(width // 8):
        low = block * 8
        shape = (rows - low, width)
        lane = lax.broadcasted_iota(jnp.int32, shape, 1)
        row = lax.broadcasted_iota(jnp.int32, shape, 0) + low
        parts = [out_ref[m, low:, :] for m in range(mats)]
        for t in range(8):
            j = low + t
            pick = lane == j
            later = lane > j
            for m in range(mats):
                a = parts[m]
                pivot_row = a[t : t + 1]
                pivot = jnp.sum(jnp.where(pick[:1], pivot_row, 0.0), axis=1, keepdims=True)
                scale = 1.0 / jnp.sqrt(pivot)
                column = jnp.sum(jnp.where(pick, a, 0.0), axis=1, keepdims=True) * scale
                column = jnp.where(row[:, :1] >= j, column, 0.0)
                updated = a - column * (pivot_row * scale)
                parts[m] = jnp.where(later, updated, jnp.where(pick, column, a))
        for m in range(mats):
            out_ref[m, low:, :] = parts[m]
    lane = lax.broadcasted_iota(jnp.int32, (rows, width), 1)
    row = lax.broadcasted_iota(jnp.int32, (rows, width), 0)
    for m in range(mats):
        out_ref[m] = jnp.where(row >= lane, out_ref[m], 0.0)


def cholesky_rows(stacked):
    vmem = pltpu.MemorySpace.VMEM
    return pl.pallas_call(
        cholesky_kernel,
        out_shape=jax.ShapeDtypeStruct(stacked.shape, jnp.float32),
        in_specs=[pl.BlockSpec(memory_space=vmem)],
        out_specs=pl.BlockSpec(memory_space=vmem),
    )(stacked)


def on_device(leaf_points, col_points, source_hash_signs, adjacent_leaf_lists, near_count):
    owned = lax.all_gather(col_points, "row", axis=1, tiled=True)
    leaves = leaf_points.shape[0]
    pair_count = near_count[:, 0]
    samples = accumulate(
        leaf_points,
        owned.reshape(owned.shape[1:]),
        source_hash_signs.reshape(source_hash_signs.shape[1:]),
        adjacent_leaf_lists,
        pair_count,
    )
    for bit in range(lax.axis_size("col").bit_length() - 1):
        samples = samples + from_partner(samples, "col", bit)
    rows = samples.shape[1] // lax.axis_size("col")
    rows_part = lax.dynamic_slice_in_dim(samples, lax.axis_index("col") * rows, rows, axis=1)
    gram = jnp.einsum("bri,brk->bik", samples, samples, precision=lax.Precision.HIGHEST)
    ridge = jnp.trace(gram, axis1=1, axis2=2) / SK + ridge_eps
    shifted = gram + ridge[:, None, None] * jnp.eye(SK, dtype=jnp.float32)[None]
    total = jnp.sum(shifted, axis=0)
    local_levels = leaves.bit_length() - 1
    for bit in range(MERGED_LEVELS - local_levels):
        total = total + from_partner(total, "row", bit)
    stacked = jnp.concatenate(
        [
            jnp.concatenate([shifted, rows_part], axis=1),
            jnp.concatenate([total, jnp.zeros_like(rows_part[0])], axis=0)[None],
        ],
        axis=0,
    )
    factored = cholesky_rows(stacked)
    leaf_basis = factored[:leaves, SK:, :]
    factor = jnp.swapaxes(factored[leaves:, :SK, :], 1, 2)
    return (leaf_basis, factor)


def solution(mesh):
    return jax.shard_map(
        on_device,
        mesh=mesh,
        in_specs=(
            P("row", None, None),
            P("col", "row", None, None),
            P("col", None, None),
            P("row", "col"),
            P("row", "col"),
        ),
        out_specs=(P("row", "col", None), P("row", None, None)),
        check_vma=False,
    )
```

```python
from functools import partial

import jax
import jax.numpy as jnp
from jax import lax
from jax.sharding import PartitionSpec as P
from jax.experimental import pallas as pl
from jax.experimental.pallas import tpu as pltpu

SK = 128
MERGED_LEVELS = 4


half_inverse = 0.125
ridge_eps = 1e-05


def from_partner(value, axis, stride):
    mask = 2**stride
    pairs = [(source, source ^ mask) for source in range(lax.axis_size(axis))]
    return lax.ppermute(value, axis, pairs)


def split3(value):
    first = value.astype(jnp.bfloat16)
    rest = value - first.astype(jnp.float32)
    second = rest.astype(jnp.bfloat16)
    third = (rest - second.astype(jnp.float32)).astype(jnp.bfloat16)
    return first, second, third


def row_operand(leaf_points):
    norms = jnp.sum(leaf_points * leaf_points, axis=1)
    scaled = jnp.swapaxes(leaf_points, 1, 2) * (2.0 * half_inverse)
    place = lax.broadcasted_iota(jnp.int32, norms.shape + (8,), 2)
    tail = jnp.where(place == 0, -half_inverse, jnp.where(place == 1, -half_inverse * norms[:, :, None], 0.0))
    first, second, third = split3(jnp.concatenate([scaled, tail], axis=2))
    return jnp.concatenate([first, first, second, second, first, third], axis=2)


def sketch_kernel(slots_ref, counts_ref, row_ref, col_ref, code_ref, *refs):
    out_ref = refs[-1]
    leaves = out_ref.shape[0]
    points = col_ref.shape[2]
    place = lax.broadcasted_iota(jnp.int32, (8, points), 0)
    bucket_id = lax.broadcasted_iota(jnp.int32, (SK, points), 0)
    contract_last = (((1,), (1,)), ((), ()))
    for leaf in range(leaves):
        out_ref[leaf] = jnp.zeros(out_ref.shape[1:], jnp.float32)

        def tile(slot, carry):
            column = slots_ref[leaf, slot]
            y = col_ref[column]
            norms = jnp.sum(y * y, axis=0, keepdims=True)
            tail = jnp.where(place == 0, norms, jnp.where(place == 1, 1.0, 0.0))
            first, second, third = split3(jnp.concatenate([y, tail], axis=0))
            stacked = jnp.concatenate([first, second, first, second, third, first], axis=0)
            exponent = jnp.dot(row_ref[leaf], stacked, preferred_element_type=jnp.float32)
            kernel = jnp.exp(exponent)
            code = code_ref[pl.ds(column, 1), :]
            signs = (1 - 2 * (code // SK)).astype(jnp.float32)
            omega_t = jnp.where(bucket_id == code % SK, signs, 0.0).astype(jnp.bfloat16)
            high = kernel.astype(jnp.bfloat16)
            low = (kernel - high.astype(jnp.float32)).astype(jnp.bfloat16)
            terms = lax.dot_general(high, omega_t, contract_last, preferred_element_type=jnp.float32)
            terms = terms + lax.dot_general(low, omega_t, contract_last, preferred_element_type=jnp.float32)
            out_ref[leaf] += terms
            return carry

        def two_tiles(step, carry):
            return tile(2 * step + 1, tile(2 * step, carry))

        count = counts_ref[leaf]
        lax.fori_loop(0, count // 2, two_tiles, 0)
        lax.fori_loop((count // 2) * 2, count, tile, 0)


def accumulate(leaf_points, col_store, code_store, slot_table, pair_count, after=()):
    leaves, _, points = leaf_points.shape
    smem, vmem = pltpu.MemorySpace.SMEM, pltpu.MemorySpace.VMEM
    return pl.pallas_call(
        sketch_kernel,
        out_shape=jax.ShapeDtypeStruct((leaves, points, SK), jnp.float32),
        in_specs=[pl.BlockSpec(memory_space=smem)] * 2
        + [pl.BlockSpec(memory_space=vmem)] * 3
        + [pl.BlockSpec(memory_space=pl.ANY)] * len(after),
        out_specs=pl.BlockSpec(memory_space=vmem),
        compiler_params=pltpu.CompilerParams(vmem_limit_bytes=48 * 1024 * 1024),
        cost_estimate=pl.CostEstimate(
            flops=int(slot_table.size) * points * points * (96 + 4 * SK) * 2,
            transcendentals=int(slot_table.size) * points * points,
            bytes_accessed=int(slot_table.size) * points * 40 + leaves * points * SK * 4,
        ),
    )(slot_table, pair_count, row_operand(leaf_points), col_store, code_store, *after)


def cholesky_kernel(in_ref, out_ref):
    mats, rows, width = in_ref.shape
    out_ref[...] = in_ref[...]
    for block in range(width // 8):
        low = block * 8
        shape = (rows - low, width)
        lane = lax.broadcasted_iota(jnp.int32, shape, 1)
        row = lax.broadcasted_iota(jnp.int32, shape, 0) + low
        parts = [out_ref[m, low:, :] for m in range(mats)]
        for t in range(8):
            j = low + t
            pick = lane == j
            later = lane > j
            for m in range(mats):
                a = parts[m]
                pivot_row = a[t : t + 1]
                pivot = jnp.sum(jnp.where(pick[:1], pivot_row, 0.0), axis=1, keepdims=True)
                scale = 1.0 / jnp.sqrt(pivot)
                column = jnp.sum(jnp.where(pick, a, 0.0), axis=1, keepdims=True) * scale
                column = jnp.where(row[:, :1] >= j, column, 0.0)
                updated = a - column * (pivot_row * scale)
                parts[m] = jnp.where(later, updated, jnp.where(pick, column, a))
        for m in range(mats):
            out_ref[m, low:, :] = parts[m]
    lane = lax.broadcasted_iota(jnp.int32, (rows, width), 1)
    row = lax.broadcasted_iota(jnp.int32, (rows, width), 0)
    for m in range(mats):
        out_ref[m] = jnp.where(row >= lane, out_ref[m], 0.0)


def cholesky_rows(stacked):
    vmem = pltpu.MemorySpace.VMEM
    return pl.pallas_call(
        cholesky_kernel,
        out_shape=jax.ShapeDtypeStruct(stacked.shape, jnp.float32),
        in_specs=[pl.BlockSpec(memory_space=vmem)],
        out_specs=pl.BlockSpec(memory_space=vmem),
    )(stacked)


def on_device(leaf_points, col_points, source_hash_signs, adjacent_leaf_lists, near_count):
    owned = lax.all_gather(col_points, "row", axis=1, tiled=True)
    leaves = leaf_points.shape[0]
    pair_count = near_count[:, 0]
    col_store = owned.reshape(owned.shape[1:])
    code_store = source_hash_signs.reshape(source_hash_signs.shape[1:])
    steps = lax.axis_size("col").bit_length() - 1
    per_leaf, taken = [], []

    def advance(e, upto):
        while taken[e] < min(upto, steps):
            per_leaf[e] = per_leaf[e] + from_partner(per_leaf[e], "col", taken[e])
            taken[e] += 1

    for leaf in range(leaves):
        for e in range(leaf):
            advance(e, leaf - 1 - e)
        after = tuple(per_leaf[e] for e in range(leaf) if taken[e] > 0)
        per_leaf.append(
            accumulate(
                leaf_points[leaf : leaf + 1],
                col_store,
                code_store,
                adjacent_leaf_lists[leaf : leaf + 1],
                pair_count[leaf : leaf + 1],
                after,
            )
        )
        taken.append(0)
    for e in range(leaves):
        advance(e, steps)
    samples = jnp.concatenate(per_leaf, axis=0)
    rows = samples.shape[1] // lax.axis_size("col")
    rows_part = lax.dynamic_slice_in_dim(samples, lax.axis_index("col") * rows, rows, axis=1)
    gram = jnp.einsum("bri,brk->bik", samples, samples, precision=lax.Precision.HIGHEST)
    ridge = jnp.trace(gram, axis1=1, axis2=2) / SK + ridge_eps
    shifted = gram + ridge[:, None, None] * jnp.eye(SK, dtype=jnp.float32)[None]
    total = jnp.sum(shifted, axis=0)
    local_levels = leaves.bit_length() - 1
    for bit in range(MERGED_LEVELS - local_levels):
        total = total + from_partner(total, "row", bit)
    stacked = jnp.concatenate(
        [
            jnp.concatenate([shifted, rows_part], axis=1),
            jnp.concatenate([total, jnp.zeros_like(rows_part[0])], axis=0)[None],
        ],
        axis=0,
    )
    factored = cholesky_rows(stacked)
    leaf_basis = factored[:leaves, SK:, :]
    factor = jnp.swapaxes(factored[leaves:, :SK, :], 1, 2)
    return (leaf_basis, factor)


def solution(mesh):
    return jax.shard_map(
        on_device,
        mesh=mesh,
        in_specs=(
            P("row", None, None),
            P("col", "row", None, None),
            P("col", None, None),
            P("row", "col"),
            P("row", "col"),
        ),
        out_specs=(P("row", "col", None), P("row", None, None)),
        check_vma=False,
    )
```

```python
from functools import partial

import jax
import jax.numpy as jnp
from jax import lax
from jax.sharding import PartitionSpec as P
from jax.experimental import pallas as pl
from jax.experimental.pallas import tpu as pltpu

SK = 128
MERGED_LEVELS = 4


half_inverse = 0.125
ridge_eps = 1e-05


def from_partner(value, axis, stride):
    mask = 2**stride
    pairs = [(source, source ^ mask) for source in range(lax.axis_size(axis))]
    return lax.ppermute(value, axis, pairs)


def split3(value):
    first = value.astype(jnp.bfloat16)
    rest = value - first.astype(jnp.float32)
    second = rest.astype(jnp.bfloat16)
    third = (rest - second.astype(jnp.float32)).astype(jnp.bfloat16)
    return first, second, third


def row_operand(leaf_points):
    norms = jnp.sum(leaf_points * leaf_points, axis=1)
    scaled = jnp.swapaxes(leaf_points, 1, 2) * (2.0 * half_inverse)
    place = lax.broadcasted_iota(jnp.int32, norms.shape + (8,), 2)
    tail = jnp.where(place == 0, -half_inverse, jnp.where(place == 1, -half_inverse * norms[:, :, None], 0.0))
    first, second, third = split3(jnp.concatenate([scaled, tail], axis=2))
    return jnp.concatenate([first, first, second, second, first, third], axis=2)


def sketch_kernel(leaf_block, slots_ref, counts_ref, core_ref, row_ref, mine_ref, theirs_ref, code_ref, *refs):
    out_ref = refs[-1]
    leaves = out_ref.shape[0]
    points = mine_ref.shape[2]
    place = lax.broadcasted_iota(jnp.int32, (8, points), 0)
    bucket_id = lax.broadcasted_iota(jnp.int32, (SK, points), 0)
    contract_last = (((1,), (1,)), ((), ()))
    for leaf in range(leaves):
        out_ref[leaf] = jnp.zeros(out_ref.shape[1:], jnp.float32)

        def tile(slot, carry):
            column = slots_ref[leaf, slot]
            index = (column // (2 * leaf_block)) * leaf_block + column % leaf_block
            same = (column // leaf_block) % 2 == core_ref[0]
            y = jnp.where(same, mine_ref[index], theirs_ref[index])
            norms = jnp.sum(y * y, axis=0, keepdims=True)
            tail = jnp.where(place == 0, norms, jnp.where(place == 1, 1.0, 0.0))
            first, second, third = split3(jnp.concatenate([y, tail], axis=0))
            stacked = jnp.concatenate([first, second, first, second, third, first], axis=0)
            exponent = jnp.dot(row_ref[leaf], stacked, preferred_element_type=jnp.float32)
            kernel = jnp.exp(exponent)
            code = code_ref[pl.ds(column, 1), :]
            signs = (1 - 2 * (code // SK)).astype(jnp.float32)
            omega_t = jnp.where(bucket_id == code % SK, signs, 0.0).astype(jnp.bfloat16)
            high = kernel.astype(jnp.bfloat16)
            low = (kernel - high.astype(jnp.float32)).astype(jnp.bfloat16)
            terms = lax.dot_general(high, omega_t, contract_last, preferred_element_type=jnp.float32)
            terms = terms + lax.dot_general(low, omega_t, contract_last, preferred_element_type=jnp.float32)
            out_ref[leaf] += terms
            return carry

        def two_tiles(step, carry):
            return tile(2 * step + 1, tile(2 * step, carry))

        count = counts_ref[leaf]
        lax.fori_loop(0, count // 2, two_tiles, 0)
        lax.fori_loop((count // 2) * 2, count, tile, 0)


def accumulate(leaf_points, halves, core, leaf_block, code_store, slot_table, pair_count, after=()):
    leaves, _, points = leaf_points.shape
    smem, vmem = pltpu.MemorySpace.SMEM, pltpu.MemorySpace.VMEM
    return pl.pallas_call(
        partial(sketch_kernel, leaf_block),
        out_shape=jax.ShapeDtypeStruct((leaves, points, SK), jnp.float32),
        in_specs=[pl.BlockSpec(memory_space=smem)] * 3
        + [pl.BlockSpec(memory_space=vmem)] * 4
        + [pl.BlockSpec(memory_space=pl.ANY)] * len(after),
        out_specs=pl.BlockSpec(memory_space=vmem),
        compiler_params=pltpu.CompilerParams(vmem_limit_bytes=48 * 1024 * 1024),
        cost_estimate=pl.CostEstimate(
            flops=int(slot_table.size) * points * points * (96 + 4 * SK) * 2,
            transcendentals=int(slot_table.size) * points * points,
            bytes_accessed=int(slot_table.size) * points * 40 + leaves * points * SK * 4,
        ),
    )(slot_table, pair_count, core, row_operand(leaf_points), *halves, code_store, *after)


def cholesky_kernel(in_ref, out_ref):
    mats, rows, width = in_ref.shape
    out_ref[...] = in_ref[...]
    for block in range(width // 8):
        low = block * 8
        shape = (rows - low, width)
        lane = lax.broadcasted_iota(jnp.int32, shape, 1)
        row = lax.broadcasted_iota(jnp.int32, shape, 0) + low
        parts = [out_ref[m, low:, :] for m in range(mats)]
        for t in range(8):
            j = low + t
            pick = lane == j
            later = lane > j
            for m in range(mats):
                a = parts[m]
                pivot_row = a[t : t + 1]
                pivot = jnp.sum(jnp.where(pick[:1], pivot_row, 0.0), axis=1, keepdims=True)
                scale = 1.0 / jnp.sqrt(pivot)
                column = jnp.sum(jnp.where(pick, a, 0.0), axis=1, keepdims=True) * scale
                column = jnp.where(row[:, :1] >= j, column, 0.0)
                updated = a - column * (pivot_row * scale)
                parts[m] = jnp.where(later, updated, jnp.where(pick, column, a))
        for m in range(mats):
            out_ref[m, low:, :] = parts[m]
    lane = lax.broadcasted_iota(jnp.int32, (rows, width), 1)
    row = lax.broadcasted_iota(jnp.int32, (rows, width), 0)
    for m in range(mats):
        out_ref[m] = jnp.where(row >= lane, out_ref[m], 0.0)


def cholesky_rows(stacked):
    vmem = pltpu.MemorySpace.VMEM
    return pl.pallas_call(
        cholesky_kernel,
        out_shape=jax.ShapeDtypeStruct(stacked.shape, jnp.float32),
        in_specs=[pl.BlockSpec(memory_space=vmem)],
        out_specs=pl.BlockSpec(memory_space=vmem),
    )(stacked)


def on_device(leaf_points, col_points, source_hash_signs, adjacent_leaf_lists, near_count):
    mine = lax.all_gather(col_points, "hi", axis=1, tiled=True)
    theirs = lax.ppermute(mine, "core", [(0, 1), (1, 0)])
    halves = (mine.reshape(mine.shape[1:]), theirs.reshape(theirs.shape[1:]))
    core = lax.axis_index("core").astype(jnp.int32).reshape(1)
    leaf_block = col_points.shape[1]
    leaves = leaf_points.shape[0]
    pair_count = near_count[:, 0]
    code_store = source_hash_signs.reshape(source_hash_signs.shape[1:])
    steps = lax.axis_size("col").bit_length() - 1
    per_leaf, taken = [], []

    def advance(e, upto):
        while taken[e] < min(upto, steps):
            per_leaf[e] = per_leaf[e] + from_partner(per_leaf[e], "col", taken[e])
            taken[e] += 1

    for leaf in range(leaves):
        for e in range(leaf):
            advance(e, leaf - 1 - e)
        after = tuple(per_leaf[e] for e in range(leaf) if taken[e] > 0)
        per_leaf.append(
            accumulate(
                leaf_points[leaf : leaf + 1],
                halves,
                core,
                leaf_block,
                code_store,
                adjacent_leaf_lists[leaf : leaf + 1],
                pair_count[leaf : leaf + 1],
                after,
            )
        )
        taken.append(0)
    for e in range(leaves):
        advance(e, steps)
    samples = jnp.concatenate(per_leaf, axis=0)
    rows = samples.shape[1] // lax.axis_size("col")
    rows_part = lax.dynamic_slice_in_dim(samples, lax.axis_index("col") * rows, rows, axis=1)
    gram = jnp.einsum("bri,brk->bik", samples, samples, precision=lax.Precision.HIGHEST)
    ridge = jnp.trace(gram, axis1=1, axis2=2) / SK + ridge_eps
    shifted = gram + ridge[:, None, None] * jnp.eye(SK, dtype=jnp.float32)[None]
    total = jnp.sum(shifted, axis=0)
    local_levels = leaves.bit_length() - 1
    for bit in range(MERGED_LEVELS - local_levels):
        total = total + (from_partner(total, "core", 0) if bit == 0 else from_partner(total, "hi", bit - 1))
    stacked = jnp.concatenate(
        [
            jnp.concatenate([shifted, rows_part], axis=1),
            jnp.concatenate([total, jnp.zeros_like(rows_part[0])], axis=0)[None],
        ],
        axis=0,
    )
    factored = cholesky_rows(stacked)
    leaf_basis = factored[:leaves, SK:, :]
    factor = jnp.swapaxes(factored[leaves:, :SK, :], 1, 2)
    return (leaf_basis, factor)


def solution(mesh):
    rows, cols = mesh.devices.shape
    split = jax.sharding.Mesh(mesh.devices.reshape(rows // 2, 2, cols), ("hi", "core", "col"))
    row = ("hi", "core")
    return jax.shard_map(
        on_device,
        mesh=split,
        in_specs=(
            P(row, None, None),
            P("col", row, None, None),
            P("col", None, None),
            P(row, "col"),
            P(row, "col"),
        ),
        out_specs=(P(row, "col", None), P(row, None, None)),
        check_vma=False,
    )
```

```python
from functools import partial

import jax
import jax.numpy as jnp
from jax import lax
from jax.sharding import PartitionSpec as P
from jax.experimental import pallas as pl
from jax.experimental.pallas import tpu as pltpu

SK = 128
MERGED_LEVELS = 4


half_inverse = 0.125
ridge_eps = 1e-05


def from_partner(value, axis, stride):
    mask = 2**stride
    pairs = [(source, source ^ mask) for source in range(lax.axis_size(axis))]
    return lax.ppermute(value, axis, pairs)


def split3(value):
    first = value.astype(jnp.bfloat16)
    rest = value - first.astype(jnp.float32)
    second = rest.astype(jnp.bfloat16)
    third = (rest - second.astype(jnp.float32)).astype(jnp.bfloat16)
    return first, second, third


def row_operand(leaf_points):
    norms = jnp.sum(leaf_points * leaf_points, axis=1)
    scaled = jnp.swapaxes(leaf_points, 1, 2) * (2.0 * half_inverse)
    place = lax.broadcasted_iota(jnp.int32, norms.shape + (8,), 2)
    tail = jnp.where(place == 0, -half_inverse, jnp.where(place == 1, -half_inverse * norms[:, :, None], 0.0))
    first, second, third = split3(jnp.concatenate([scaled, tail], axis=2))
    return jnp.concatenate([first, first, second, second, first, third], axis=2)


def sketch_kernel(slots_ref, counts_ref, row_ref, col_ref, code_ref, *refs):
    out_ref = refs[-1]
    leaves = out_ref.shape[0]
    points = col_ref.shape[2]
    place = lax.broadcasted_iota(jnp.int32, (8, points), 0)
    bucket_id = lax.broadcasted_iota(jnp.int32, (SK, points), 0)
    contract_last = (((1,), (1,)), ((), ()))
    for leaf in range(leaves):
        out_ref[leaf] = jnp.zeros(out_ref.shape[1:], jnp.float32)

        def tile(slot, carry):
            column = slots_ref[leaf, slot]
            y = col_ref[column]
            norms = jnp.sum(y * y, axis=0, keepdims=True)
            tail = jnp.where(place == 0, norms, jnp.where(place == 1, 1.0, 0.0))
            first, second, third = split3(jnp.concatenate([y, tail], axis=0))
            stacked = jnp.concatenate([first, second, first, second, third, first], axis=0)
            exponent = jnp.dot(row_ref[leaf], stacked, preferred_element_type=jnp.float32)
            kernel = jnp.exp(exponent)
            code = code_ref[pl.ds(column, 1), :]
            signs = (1 - 2 * (code // SK)).astype(jnp.float32)
            omega_t = jnp.where(bucket_id == code % SK, signs, 0.0).astype(jnp.bfloat16)
            high = kernel.astype(jnp.bfloat16)
            low = (kernel - high.astype(jnp.float32)).astype(jnp.bfloat16)
            terms = lax.dot_general(high, omega_t, contract_last, preferred_element_type=jnp.float32)
            terms = terms + lax.dot_general(low, omega_t, contract_last, preferred_element_type=jnp.float32)
            out_ref[leaf] += terms
            return carry

        def two_tiles(step, carry):
            return tile(2 * step + 1, tile(2 * step, carry))

        count = counts_ref[leaf]
        lax.fori_loop(0, count // 2, two_tiles, 0)
        lax.fori_loop((count // 2) * 2, count, tile, 0)


def accumulate(leaf_points, col_store, code_store, slot_table, pair_count, after=()):
    leaves, _, points = leaf_points.shape
    smem, vmem = pltpu.MemorySpace.SMEM, pltpu.MemorySpace.VMEM
    return pl.pallas_call(
        sketch_kernel,
        out_shape=jax.ShapeDtypeStruct((leaves, points, SK), jnp.float32),
        in_specs=[pl.BlockSpec(memory_space=smem)] * 2
        + [pl.BlockSpec(memory_space=vmem)] * 3
        + [pl.BlockSpec(memory_space=pl.ANY)] * len(after),
        out_specs=pl.BlockSpec(memory_space=vmem),
        compiler_params=pltpu.CompilerParams(vmem_limit_bytes=48 * 1024 * 1024),
        cost_estimate=pl.CostEstimate(
            flops=int(slot_table.size) * points * points * (96 + 4 * SK) * 2,
            transcendentals=int(slot_table.size) * points * points,
            bytes_accessed=int(slot_table.size) * points * 40 + leaves * points * SK * 4,
        ),
    )(slot_table, pair_count, row_operand(leaf_points), col_store, code_store, *after)


def cholesky_kernel(in_ref, out_ref):
    mats, rows, width = in_ref.shape
    out_ref[...] = in_ref[...]
    for block in range(width // 8):
        low = block * 8
        shape = (rows - low, width)
        lane = lax.broadcasted_iota(jnp.int32, shape, 1)
        row = lax.broadcasted_iota(jnp.int32, shape, 0) + low
        parts = [out_ref[m, low:, :] for m in range(mats)]
        for t in range(8):
            j = low + t
            pick = lane == j
            later = lane > j
            for m in range(mats):
                a = parts[m]
                pivot_row = a[t : t + 1]
                pivot = jnp.sum(jnp.where(pick[:1], pivot_row, 0.0), axis=1, keepdims=True)
                scale = 1.0 / jnp.sqrt(pivot)
                column = jnp.sum(jnp.where(pick, a, 0.0), axis=1, keepdims=True) * scale
                column = jnp.where(row[:, :1] >= j, column, 0.0)
                updated = a - column * (pivot_row * scale)
                parts[m] = jnp.where(later, updated, jnp.where(pick, column, a))
        for m in range(mats):
            out_ref[m, low:, :] = parts[m]
    lane = lax.broadcasted_iota(jnp.int32, (rows, width), 1)
    row = lax.broadcasted_iota(jnp.int32, (rows, width), 0)
    for m in range(mats):
        out_ref[m] = jnp.where(row >= lane, out_ref[m], 0.0)


def cholesky_rows(stacked):
    vmem = pltpu.MemorySpace.VMEM
    return pl.pallas_call(
        cholesky_kernel,
        out_shape=jax.ShapeDtypeStruct(stacked.shape, jnp.float32),
        in_specs=[pl.BlockSpec(memory_space=vmem)],
        out_specs=pl.BlockSpec(memory_space=vmem),
    )(stacked)


def on_device(leaf_points, col_points, source_hash_signs, adjacent_leaf_lists, near_count):
    copies = jnp.broadcast_to(col_points, (lax.axis_size("row"),) + col_points.shape)
    owned = lax.all_to_all(copies, "row", 0, 0, tiled=True).reshape((1, -1) + col_points.shape[2:])
    leaves = leaf_points.shape[0]
    pair_count = near_count[:, 0]
    col_store = owned.reshape(owned.shape[1:])
    code_store = source_hash_signs.reshape(source_hash_signs.shape[1:])
    steps = lax.axis_size("col").bit_length() - 1
    per_leaf, taken = [], []

    def advance(e, upto):
        while taken[e] < min(upto, steps):
            per_leaf[e] = per_leaf[e] + from_partner(per_leaf[e], "col", taken[e])
            taken[e] += 1

    for leaf in range(leaves):
        for e in range(leaf):
            advance(e, leaf - 1 - e)
        after = tuple(per_leaf[e] for e in range(leaf) if taken[e] > 0)
        per_leaf.append(
            accumulate(
                leaf_points[leaf : leaf + 1],
                col_store,
                code_store,
                adjacent_leaf_lists[leaf : leaf + 1],
                pair_count[leaf : leaf + 1],
                after,
            )
        )
        taken.append(0)
    for e in range(leaves):
        advance(e, steps)
    samples = jnp.concatenate(per_leaf, axis=0)
    rows = samples.shape[1] // lax.axis_size("col")
    rows_part = lax.dynamic_slice_in_dim(samples, lax.axis_index("col") * rows, rows, axis=1)
    gram = jnp.einsum("bri,brk->bik", samples, samples, precision=lax.Precision.HIGHEST)
    ridge = jnp.trace(gram, axis1=1, axis2=2) / SK + ridge_eps
    shifted = gram + ridge[:, None, None] * jnp.eye(SK, dtype=jnp.float32)[None]
    total = jnp.sum(shifted, axis=0)
    local_levels = leaves.bit_length() - 1
    for bit in range(MERGED_LEVELS - local_levels):
        total = total + from_partner(total, "row", bit)
    stacked = jnp.concatenate(
        [
            jnp.concatenate([shifted, rows_part], axis=1),
            jnp.concatenate([total, jnp.zeros_like(rows_part[0])], axis=0)[None],
        ],
        axis=0,
    )
    factored = cholesky_rows(stacked)
    leaf_basis = factored[:leaves, SK:, :]
    factor = jnp.swapaxes(factored[leaves:, :SK, :], 1, 2)
    return (leaf_basis, factor)


def solution(mesh):
    return jax.shard_map(
        on_device,
        mesh=mesh,
        in_specs=(
            P("row", None, None),
            P("col", "row", None, None),
            P("col", None, None),
            P("row", "col"),
            P("row", "col"),
        ),
        out_specs=(P("row", "col", None), P("row", None, None)),
        check_vma=False,
    )
```

```python
from functools import partial

import jax
import jax.numpy as jnp
from jax import lax
from jax.sharding import PartitionSpec as P
from jax.experimental import pallas as pl
from jax.experimental.pallas import tpu as pltpu

SK = 128
MERGED_LEVELS = 4


half_inverse = 0.125
ridge_eps = 1e-05


def from_partner(value, axis, stride):
    mask = 2**stride
    pairs = [(source, source ^ mask) for source in range(lax.axis_size(axis))]
    return lax.ppermute(value, axis, pairs)


def split3(value):
    first = value.astype(jnp.bfloat16)
    rest = value - first.astype(jnp.float32)
    second = rest.astype(jnp.bfloat16)
    third = (rest - second.astype(jnp.float32)).astype(jnp.bfloat16)
    return first, second, third


def row_operand(leaf_points):
    norms = jnp.sum(leaf_points * leaf_points, axis=1)
    scaled = jnp.swapaxes(leaf_points, 1, 2) * (2.0 * half_inverse)
    place = lax.broadcasted_iota(jnp.int32, norms.shape + (8,), 2)
    tail = jnp.where(place == 0, -half_inverse, jnp.where(place == 1, -half_inverse * norms[:, :, None], 0.0))
    first, second, third = split3(jnp.concatenate([scaled, tail], axis=2))
    return jnp.concatenate([first, first, second, second, first, third], axis=2)


def sketch_kernel(slots_ref, counts_ref, row_ref, col_ref, code_ref, *refs):
    out_ref = refs[-1]
    leaves = out_ref.shape[0]
    points = col_ref.shape[2]
    place = lax.broadcasted_iota(jnp.int32, (8, points), 0)
    bucket_id = lax.broadcasted_iota(jnp.int32, (SK, points), 0)
    contract_last = (((1,), (1,)), ((), ()))
    for leaf in range(leaves):
        out_ref[leaf] = jnp.zeros(out_ref.shape[1:], jnp.float32)

        def tile(slot, carry):
            column = slots_ref[leaf, slot]
            y = col_ref[column]
            norms = jnp.sum(y * y, axis=0, keepdims=True)
            tail = jnp.where(place == 0, norms, jnp.where(place == 1, 1.0, 0.0))
            first, second, third = split3(jnp.concatenate([y, tail], axis=0))
            stacked = jnp.concatenate([first, second, first, second, third, first], axis=0)
            exponent = jnp.dot(row_ref[leaf], stacked, preferred_element_type=jnp.float32)
            kernel = jnp.exp(exponent)
            code = code_ref[pl.ds(column, 1), :]
            signs = (1 - 2 * (code // SK)).astype(jnp.float32)
            omega_t = jnp.where(bucket_id == code % SK, signs, 0.0).astype(jnp.bfloat16)
            high = kernel.astype(jnp.bfloat16)
            low = (kernel - high.astype(jnp.float32)).astype(jnp.bfloat16)
            terms = lax.dot_general(high, omega_t, contract_last, preferred_element_type=jnp.float32)
            terms = terms + lax.dot_general(low, omega_t, contract_last, preferred_element_type=jnp.float32)
            out_ref[leaf] += terms
            return carry

        def two_tiles(step, carry):
            return tile(2 * step + 1, tile(2 * step, carry))

        count = counts_ref[leaf]
        lax.fori_loop(0, count // 2, two_tiles, 0)
        lax.fori_loop((count // 2) * 2, count, tile, 0)


def accumulate(row_op, col_store, code_store, slot_table, pair_count, after=()):
    leaves, points, _ = row_op.shape
    smem, vmem = pltpu.MemorySpace.SMEM, pltpu.MemorySpace.VMEM
    return pl.pallas_call(
        sketch_kernel,
        out_shape=jax.ShapeDtypeStruct((leaves, points, SK), jnp.float32),
        in_specs=[pl.BlockSpec(memory_space=smem)] * 2
        + [pl.BlockSpec(memory_space=vmem)] * 3
        + [pl.BlockSpec(memory_space=pl.ANY)] * len(after),
        out_specs=pl.BlockSpec(memory_space=vmem),
        compiler_params=pltpu.CompilerParams(vmem_limit_bytes=48 * 1024 * 1024),
        cost_estimate=pl.CostEstimate(
            flops=int(slot_table.size) * points * col_store.shape[2] * (96 + 4 * SK) * 2,
            transcendentals=int(slot_table.size) * points * col_store.shape[2],
            bytes_accessed=int(slot_table.size) * points * 40 + leaves * points * SK * 4,
        ),
    )(slot_table, pair_count, row_op, col_store, code_store, *after)


def cholesky_kernel(in_ref, out_ref):
    mats, rows, width = in_ref.shape
    out_ref[...] = in_ref[...]
    for block in range(width // 8):
        low = block * 8
        shape = (rows - low, width)
        lane = lax.broadcasted_iota(jnp.int32, shape, 1)
        row = lax.broadcasted_iota(jnp.int32, shape, 0) + low
        parts = [out_ref[m, low:, :] for m in range(mats)]
        for t in range(8):
            j = low + t
            pick = lane == j
            later = lane > j
            for m in range(mats):
                a = parts[m]
                pivot_row = a[t : t + 1]
                pivot = jnp.sum(jnp.where(pick[:1], pivot_row, 0.0), axis=1, keepdims=True)
                scale = 1.0 / jnp.sqrt(pivot)
                column = jnp.sum(jnp.where(pick, a, 0.0), axis=1, keepdims=True) * scale
                column = jnp.where(row[:, :1] >= j, column, 0.0)
                updated = a - column * (pivot_row * scale)
                parts[m] = jnp.where(later, updated, jnp.where(pick, column, a))
        for m in range(mats):
            out_ref[m, low:, :] = parts[m]
    lane = lax.broadcasted_iota(jnp.int32, (rows, width), 1)
    row = lax.broadcasted_iota(jnp.int32, (rows, width), 0)
    for m in range(mats):
        out_ref[m] = jnp.where(row >= lane, out_ref[m], 0.0)


def cholesky_rows(stacked):
    vmem = pltpu.MemorySpace.VMEM
    return pl.pallas_call(
        cholesky_kernel,
        out_shape=jax.ShapeDtypeStruct(stacked.shape, jnp.float32),
        in_specs=[pl.BlockSpec(memory_space=vmem)],
        out_specs=pl.BlockSpec(memory_space=vmem),
    )(stacked)


def on_device(leaf_points, col_points, source_hash_signs, adjacent_leaf_lists, near_count):
    copies = jnp.broadcast_to(col_points, (lax.axis_size("row"),) + col_points.shape)
    owned = lax.all_to_all(copies, "row", 0, 0, tiled=True).reshape((1, -1) + col_points.shape[2:])
    leaves = leaf_points.shape[0]
    pair_count = near_count[:, 0]
    col_store = owned.reshape(owned.shape[1:])
    code_store = source_hash_signs.reshape(source_hash_signs.shape[1:])
    row_op = row_operand(leaf_points)
    halves = 2
    span = row_op.shape[1] // halves
    steps = lax.axis_size("col").bit_length() - 1
    per_part, taken = [], []

    def advance(e, upto):
        while taken[e] < min(upto, steps):
            per_part[e] = per_part[e] + from_partner(per_part[e], "col", taken[e])
            taken[e] += 1

    for part in range(leaves * halves):
        leaf, half = divmod(part, halves)
        for e in range(part):
            advance(e, part - 1 - e)
        after = tuple(per_part[e] for e in range(part) if taken[e] > 0)
        per_part.append(
            accumulate(
                row_op[leaf : leaf + 1, half * span : (half + 1) * span],
                col_store,
                code_store,
                adjacent_leaf_lists[leaf : leaf + 1],
                pair_count[leaf : leaf + 1],
                after,
            )
        )
        taken.append(0)
    for e in range(leaves * halves):
        advance(e, steps)
    per_leaf = [
        jnp.concatenate(per_part[leaf * halves : (leaf + 1) * halves], axis=1) for leaf in range(leaves)
    ]
    samples = jnp.concatenate(per_leaf, axis=0)
    rows = samples.shape[1] // lax.axis_size("col")
    rows_part = lax.dynamic_slice_in_dim(samples, lax.axis_index("col") * rows, rows, axis=1)
    gram = jnp.einsum("bri,brk->bik", samples, samples, precision=lax.Precision.HIGHEST)
    ridge = jnp.trace(gram, axis1=1, axis2=2) / SK + ridge_eps
    shifted = gram + ridge[:, None, None] * jnp.eye(SK, dtype=jnp.float32)[None]
    total = jnp.sum(shifted, axis=0)
    local_levels = leaves.bit_length() - 1
    for bit in range(MERGED_LEVELS - local_levels):
        total = total + from_partner(total, "row", bit)
    stacked = jnp.concatenate(
        [
            jnp.concatenate([shifted, rows_part], axis=1),
            jnp.concatenate([total, jnp.zeros_like(rows_part[0])], axis=0)[None],
        ],
        axis=0,
    )
    factored = cholesky_rows(stacked)
    leaf_basis = factored[:leaves, SK:, :]
    factor = jnp.swapaxes(factored[leaves:, :SK, :], 1, 2)
    return (leaf_basis, factor)


def solution(mesh):
    return jax.shard_map(
        on_device,
        mesh=mesh,
        in_specs=(
            P("row", None, None),
            P("col", "row", None, None),
            P("col", None, None),
            P("row", "col"),
            P("row", "col"),
        ),
        out_specs=(P("row", "col", None), P("row", None, None)),
        check_vma=False,
    )
```

```python
from functools import partial

import jax
import jax.numpy as jnp
from jax import lax
from jax.sharding import PartitionSpec as P
from jax.experimental import pallas as pl
from jax.experimental.pallas import tpu as pltpu

SK = 128
MERGED_LEVELS = 4


half_inverse = 0.125
ridge_eps = 1e-05


def from_partner(value, axis, stride):
    mask = 2**stride
    pairs = [(source, source ^ mask) for source in range(lax.axis_size(axis))]
    return lax.ppermute(value, axis, pairs)


def split3(value):
    first = value.astype(jnp.bfloat16)
    rest = value - first.astype(jnp.float32)
    second = rest.astype(jnp.bfloat16)
    third = (rest - second.astype(jnp.float32)).astype(jnp.bfloat16)
    return first, second, third


def row_operand(leaf_points):
    norms = jnp.sum(leaf_points * leaf_points, axis=1)
    scaled = jnp.swapaxes(leaf_points, 1, 2) * (2.0 * half_inverse)
    place = lax.broadcasted_iota(jnp.int32, norms.shape + (8,), 2)
    tail = jnp.where(place == 0, -half_inverse, jnp.where(place == 1, -half_inverse * norms[:, :, None], 0.0))
    first, second, third = split3(jnp.concatenate([scaled, tail], axis=2))
    return jnp.concatenate([first, first, second, second, first, third], axis=2)


def sketch_kernel(shard, piece, first, slots_ref, counts_ref, row_ref, col_ref, code_ref, *refs):
    out_ref = refs[-1]
    leaves = out_ref.shape[0]
    points = col_ref.shape[2]
    place = lax.broadcasted_iota(jnp.int32, (8, points), 0)
    bucket_id = lax.broadcasted_iota(jnp.int32, (SK, points), 0)
    contract_last = (((1,), (1,)), ((), ()))
    for leaf in range(leaves):
        if first == 0:
            out_ref[leaf] = jnp.zeros(out_ref.shape[1:], jnp.float32)

        def tile(slot, carry):
            column = slots_ref[leaf, slot]
            offset = column % shard - first

            @pl.when((offset >= 0) & (offset < piece))
            def _():
                add_tile(column, (column // shard) * piece + offset)

            return carry

        def add_tile(column, index):
            y = col_ref[index]
            norms = jnp.sum(y * y, axis=0, keepdims=True)
            tail = jnp.where(place == 0, norms, jnp.where(place == 1, 1.0, 0.0))
            first, second, third = split3(jnp.concatenate([y, tail], axis=0))
            stacked = jnp.concatenate([first, second, first, second, third, first], axis=0)
            exponent = jnp.dot(row_ref[leaf], stacked, preferred_element_type=jnp.float32)
            kernel = jnp.exp(exponent)
            code = code_ref[pl.ds(column, 1), :]
            signs = (1 - 2 * (code // SK)).astype(jnp.float32)
            omega_t = jnp.where(bucket_id == code % SK, signs, 0.0).astype(jnp.bfloat16)
            high = kernel.astype(jnp.bfloat16)
            low = (kernel - high.astype(jnp.float32)).astype(jnp.bfloat16)
            terms = lax.dot_general(high, omega_t, contract_last, preferred_element_type=jnp.float32)
            terms = terms + lax.dot_general(low, omega_t, contract_last, preferred_element_type=jnp.float32)
            out_ref[leaf] += terms

        def two_tiles(step, carry):
            return tile(2 * step + 1, tile(2 * step, carry))

        count = counts_ref[leaf]
        lax.fori_loop(0, count // 2, two_tiles, 0)
        lax.fori_loop((count // 2) * 2, count, tile, 0)


def accumulate(leaf_points, col_store, code_store, slot_table, pair_count, shard, first, start=None, after=()):
    piece = col_store.shape[0] * shard // code_store.shape[0]
    leaves, _, points = leaf_points.shape
    smem, vmem = pltpu.MemorySpace.SMEM, pltpu.MemorySpace.VMEM
    return pl.pallas_call(
        partial(sketch_kernel, shard, piece, first),
        out_shape=jax.ShapeDtypeStruct((leaves, points, SK), jnp.float32),
        in_specs=[pl.BlockSpec(memory_space=smem)] * 2
        + [pl.BlockSpec(memory_space=vmem)] * 3
        + [pl.BlockSpec(memory_space=vmem)] * (start is not None)
        + [pl.BlockSpec(memory_space=pl.ANY)] * len(after),
        out_specs=pl.BlockSpec(memory_space=vmem),
        input_output_aliases={} if start is None else {5: 0},
        compiler_params=pltpu.CompilerParams(vmem_limit_bytes=48 * 1024 * 1024),
        cost_estimate=pl.CostEstimate(
            flops=int(slot_table.size) * points * points * (96 + 4 * SK) * 2,
            transcendentals=int(slot_table.size) * points * points,
            bytes_accessed=int(slot_table.size) * points * 40 + leaves * points * SK * 4,
        ),
    )(slot_table, pair_count, row_operand(leaf_points), col_store, code_store, *((start,) if start is not None else ()), *after)


def cholesky_kernel(in_ref, out_ref):
    mats, rows, width = in_ref.shape
    out_ref[...] = in_ref[...]
    for block in range(width // 8):
        low = block * 8
        shape = (rows - low, width)
        lane = lax.broadcasted_iota(jnp.int32, shape, 1)
        row = lax.broadcasted_iota(jnp.int32, shape, 0) + low
        parts = [out_ref[m, low:, :] for m in range(mats)]
        for t in range(8):
            j = low + t
            pick = lane == j
            later = lane > j
            for m in range(mats):
                a = parts[m]
                pivot_row = a[t : t + 1]
                pivot = jnp.sum(jnp.where(pick[:1], pivot_row, 0.0), axis=1, keepdims=True)
                scale = 1.0 / jnp.sqrt(pivot)
                column = jnp.sum(jnp.where(pick, a, 0.0), axis=1, keepdims=True) * scale
                column = jnp.where(row[:, :1] >= j, column, 0.0)
                updated = a - column * (pivot_row * scale)
                parts[m] = jnp.where(later, updated, jnp.where(pick, column, a))
        for m in range(mats):
            out_ref[m, low:, :] = parts[m]
    lane = lax.broadcasted_iota(jnp.int32, (rows, width), 1)
    row = lax.broadcasted_iota(jnp.int32, (rows, width), 0)
    for m in range(mats):
        out_ref[m] = jnp.where(row >= lane, out_ref[m], 0.0)


def cholesky_rows(stacked):
    vmem = pltpu.MemorySpace.VMEM
    return pl.pallas_call(
        cholesky_kernel,
        out_shape=jax.ShapeDtypeStruct(stacked.shape, jnp.float32),
        in_specs=[pl.BlockSpec(memory_space=vmem)],
        out_specs=pl.BlockSpec(memory_space=vmem),
    )(stacked)


def on_device(leaf_points, col_points, source_hash_signs, adjacent_leaf_lists, near_count):
    leaves = leaf_points.shape[0]
    shard = col_points.shape[1]
    piece = shard // 2
    devices = lax.axis_size("row")

    def gather(part):
        copies = jnp.broadcast_to(part, (devices,) + part.shape)
        return lax.all_to_all(copies, "row", 0, 0, tiled=True).reshape((-1,) + part.shape[2:])

    first_half = gather(col_points[:, :piece])
    first_half, second_part = lax.optimization_barrier((first_half, col_points[:, piece:]))
    second_half = gather(second_part)
    pair_count = near_count[:, 0]
    code_store = source_hash_signs.reshape(source_hash_signs.shape[1:])
    early = [
        accumulate(
            leaf_points[leaf : leaf + 1],
            first_half,
            code_store,
            adjacent_leaf_lists[leaf : leaf + 1],
            pair_count[leaf : leaf + 1],
            shard,
            0,
        )
        for leaf in range(leaves)
    ]
    steps = lax.axis_size("col").bit_length() - 1
    per_leaf, taken = [], []

    def advance(e, upto):
        while taken[e] < min(upto, steps):
            per_leaf[e] = per_leaf[e] + from_partner(per_leaf[e], "col", taken[e])
            taken[e] += 1

    for leaf in range(leaves):
        for e in range(leaf):
            advance(e, leaf - 1 - e)
        after = tuple(per_leaf[e] for e in range(leaf) if taken[e] > 0)
        per_leaf.append(
            accumulate(
                leaf_points[leaf : leaf + 1],
                second_half,
                code_store,
                adjacent_leaf_lists[leaf : leaf + 1],
                pair_count[leaf : leaf + 1],
                shard,
                piece,
                early[leaf],
                after,
            )
        )
        taken.append(0)
    for e in range(leaves):
        advance(e, steps)
    samples = jnp.concatenate(per_leaf, axis=0)
    rows = samples.shape[1] // lax.axis_size("col")
    rows_part = lax.dynamic_slice_in_dim(samples, lax.axis_index("col") * rows, rows, axis=1)
    gram = jnp.einsum("bri,brk->bik", samples, samples, precision=lax.Precision.HIGHEST)
    ridge = jnp.trace(gram, axis1=1, axis2=2) / SK + ridge_eps
    shifted = gram + ridge[:, None, None] * jnp.eye(SK, dtype=jnp.float32)[None]
    total = jnp.sum(shifted, axis=0)
    local_levels = leaves.bit_length() - 1
    for bit in range(MERGED_LEVELS - local_levels):
        total = total + from_partner(total, "row", bit)
    stacked = jnp.concatenate(
        [
            jnp.concatenate([shifted, rows_part], axis=1),
            jnp.concatenate([total, jnp.zeros_like(rows_part[0])], axis=0)[None],
        ],
        axis=0,
    )
    factored = cholesky_rows(stacked)
    leaf_basis = factored[:leaves, SK:, :]
    factor = jnp.swapaxes(factored[leaves:, :SK, :], 1, 2)
    return (leaf_basis, factor)


def solution(mesh):
    return jax.shard_map(
        on_device,
        mesh=mesh,
        in_specs=(
            P("row", None, None),
            P("col", "row", None, None),
            P("col", None, None),
            P("row", "col"),
            P("row", "col"),
        ),
        out_specs=(P("row", "col", None), P("row", None, None)),
        check_vma=False,
    )
```

```python
from functools import partial

import jax
import jax.numpy as jnp
from jax import lax
from jax.sharding import PartitionSpec as P
from jax.experimental import pallas as pl
from jax.experimental.pallas import tpu as pltpu

SK = 128
MERGED_LEVELS = 4


half_inverse = 0.125
ridge_eps = 1e-05


def from_partner(value, axis, stride):
    mask = 2**stride
    pairs = [(source, source ^ mask) for source in range(lax.axis_size(axis))]
    return lax.ppermute(value, axis, pairs)


def split3(value):
    first = value.astype(jnp.bfloat16)
    rest = value - first.astype(jnp.float32)
    second = rest.astype(jnp.bfloat16)
    third = (rest - second.astype(jnp.float32)).astype(jnp.bfloat16)
    return first, second, third


def row_operand(leaf_points):
    norms = jnp.sum(leaf_points * leaf_points, axis=1)
    scaled = jnp.swapaxes(leaf_points, 1, 2) * (2.0 * half_inverse)
    place = lax.broadcasted_iota(jnp.int32, norms.shape + (8,), 2)
    tail = jnp.where(place == 0, -half_inverse, jnp.where(place == 1, -half_inverse * norms[:, :, None], 0.0))
    first, second, third = split3(jnp.concatenate([scaled, tail], axis=2))
    return jnp.concatenate([first, first, second, second, first, third], axis=2)


def sketch_kernel(slots_ref, counts_ref, row_ref, col_ref, code_ref, *refs):
    out_ref = refs[-1]
    leaves = out_ref.shape[0]
    points = col_ref.shape[2]
    place = lax.broadcasted_iota(jnp.int32, (8, points), 0)
    bucket_id = lax.broadcasted_iota(jnp.int32, (SK, points), 0)
    contract_last = (((1,), (1,)), ((), ()))
    for leaf in range(leaves):
        out_ref[leaf] = jnp.zeros(out_ref.shape[1:], jnp.float32)

        def tile(slot, carry):
            column = slots_ref[leaf, slot]
            y = col_ref[column]
            norms = jnp.sum(y * y, axis=0, keepdims=True)
            tail = jnp.where(place == 0, norms, jnp.where(place == 1, 1.0, 0.0))
            first, second, third = split3(jnp.concatenate([y, tail], axis=0))
            stacked = jnp.concatenate([first, second, first, second, third, first], axis=0)
            exponent = jnp.dot(row_ref[leaf], stacked, preferred_element_type=jnp.float32)
            kernel = jnp.exp(exponent)
            code = code_ref[pl.ds(column, 1), :]
            signs = (1 - 2 * (code // SK)).astype(jnp.float32)
            omega_t = jnp.where(bucket_id == code % SK, signs, 0.0).astype(jnp.bfloat16)
            high = kernel.astype(jnp.bfloat16)
            low = (kernel - high.astype(jnp.float32)).astype(jnp.bfloat16)
            terms = lax.dot_general(high, omega_t, contract_last, preferred_element_type=jnp.float32)
            terms = terms + lax.dot_general(low, omega_t, contract_last, preferred_element_type=jnp.float32)
            out_ref[leaf] += terms
            return carry

        def two_tiles(step, carry):
            return tile(2 * step + 1, tile(2 * step, carry))

        count = counts_ref[leaf]
        lax.fori_loop(0, count // 2, two_tiles, 0)
        lax.fori_loop((count // 2) * 2, count, tile, 0)


def accumulate(leaf_points, col_store, code_store, slot_table, pair_count, after=()):
    leaves, _, points = leaf_points.shape
    smem, vmem = pltpu.MemorySpace.SMEM, pltpu.MemorySpace.VMEM
    return pl.pallas_call(
        sketch_kernel,
        out_shape=jax.ShapeDtypeStruct((leaves, points, SK), jnp.float32),
        in_specs=[pl.BlockSpec(memory_space=smem)] * 2
        + [pl.BlockSpec(memory_space=vmem)] * 3
        + [pl.BlockSpec(memory_space=pl.ANY)] * len(after),
        out_specs=pl.BlockSpec(memory_space=vmem),
        compiler_params=pltpu.CompilerParams(vmem_limit_bytes=48 * 1024 * 1024),
        cost_estimate=pl.CostEstimate(
            flops=int(slot_table.size) * points * points * (96 + 4 * SK) * 2,
            transcendentals=int(slot_table.size) * points * points,
            bytes_accessed=int(slot_table.size) * points * 40 + leaves * points * SK * 4,
        ),
    )(slot_table, pair_count, row_operand(leaf_points), col_store, code_store, *after)


def cholesky_kernel(in_ref, basis_ref, top_ref, out_ref):
    mats, rows, width = in_ref.shape
    out_ref[...] = in_ref[...]
    for block in range(width // 8):
        low = block * 8
        shape = (rows - low, width)
        lane = lax.broadcasted_iota(jnp.int32, shape, 1)
        row = lax.broadcasted_iota(jnp.int32, shape, 0) + low
        parts = [out_ref[m, low:, :] for m in range(mats)]
        for t in range(8):
            j = low + t
            pick = lane == j
            later = lane > j
            for m in range(mats):
                a = parts[m]
                pivot_row = a[t : t + 1]
                pivot = jnp.sum(jnp.where(pick[:1], pivot_row, 0.0), axis=1, keepdims=True)
                scale = 1.0 / jnp.sqrt(pivot)
                column = jnp.sum(jnp.where(pick, a, 0.0), axis=1, keepdims=True) * scale
                column = jnp.where(row[:, :1] >= j, column, 0.0)
                updated = a - column * (pivot_row * scale)
                parts[m] = jnp.where(later, updated, jnp.where(pick, column, a))
        for m in range(mats):
            out_ref[m, low:, :] = parts[m]
    leaves = basis_ref.shape[0]
    for m in range(leaves):
        basis_ref[m] = out_ref[m, width:, :]
    lane = lax.broadcasted_iota(jnp.int32, (width, width), 1)
    row = lax.broadcasted_iota(jnp.int32, (width, width), 0)
    for m in range(top_ref.shape[0]):
        top_ref[m] = jnp.where(row >= lane, out_ref[leaves + m, :width, :], 0.0).T


def cholesky_rows(stacked, leaves):
    mats, rows, width = stacked.shape
    vmem = pltpu.MemorySpace.VMEM
    return pl.pallas_call(
        cholesky_kernel,
        out_shape=(
            jax.ShapeDtypeStruct((leaves, rows - width, width), jnp.float32),
            jax.ShapeDtypeStruct((mats - leaves, width, width), jnp.float32),
        ),
        in_specs=[pl.BlockSpec(memory_space=vmem)],
        out_specs=(pl.BlockSpec(memory_space=vmem), pl.BlockSpec(memory_space=vmem)),
        scratch_shapes=[pltpu.VMEM(stacked.shape, jnp.float32)],
    )(stacked)


def on_device(leaf_points, col_points, source_hash_signs, adjacent_leaf_lists, near_count):
    copies = jnp.broadcast_to(col_points, (lax.axis_size("row"),) + col_points.shape)
    owned = lax.all_to_all(copies, "row", 0, 0, tiled=True).reshape((1, -1) + col_points.shape[2:])
    leaves = leaf_points.shape[0]
    pair_count = near_count[:, 0]
    col_store = owned.reshape(owned.shape[1:])
    code_store = source_hash_signs.reshape(source_hash_signs.shape[1:])
    steps = lax.axis_size("col").bit_length() - 1
    per_leaf, taken = [], []

    def advance(e, upto):
        while taken[e] < min(upto, steps):
            per_leaf[e] = per_leaf[e] + from_partner(per_leaf[e], "col", taken[e])
            taken[e] += 1

    for leaf in range(leaves):
        for e in range(leaf):
            advance(e, leaf - 1 - e)
        after = tuple(per_leaf[e] for e in range(leaf) if taken[e] > 0)
        per_leaf.append(
            accumulate(
                leaf_points[leaf : leaf + 1],
                col_store,
                code_store,
                adjacent_leaf_lists[leaf : leaf + 1],
                pair_count[leaf : leaf + 1],
                after,
            )
        )
        taken.append(0)
    for e in range(leaves):
        advance(e, steps)
    samples = jnp.concatenate(per_leaf, axis=0)
    rows = samples.shape[1] // lax.axis_size("col")
    rows_part = lax.dynamic_slice_in_dim(samples, lax.axis_index("col") * rows, rows, axis=1)
    gram = jnp.einsum("bri,brk->bik", samples, samples, precision=lax.Precision.HIGHEST)
    ridge = jnp.trace(gram, axis1=1, axis2=2) / SK + ridge_eps
    shifted = gram + ridge[:, None, None] * jnp.eye(SK, dtype=jnp.float32)[None]
    total = jnp.sum(shifted, axis=0)
    local_levels = leaves.bit_length() - 1
    for bit in range(MERGED_LEVELS - local_levels):
        total = total + from_partner(total, "row", bit)
    stacked = jnp.concatenate(
        [
            jnp.concatenate([shifted, rows_part], axis=1),
            jnp.concatenate([total, jnp.zeros_like(rows_part[0])], axis=0)[None],
        ],
        axis=0,
    )
    leaf_basis, factor = cholesky_rows(stacked, leaves)
    return (leaf_basis, factor)


def solution(mesh):
    return jax.shard_map(
        on_device,
        mesh=mesh,
        in_specs=(
            P("row", None, None),
            P("col", "row", None, None),
            P("col", None, None),
            P("row", "col"),
            P("row", "col"),
        ),
        out_specs=(P("row", "col", None), P("row", None, None)),
        check_vma=False,
    )
```

```python
from functools import partial

import jax
import jax.numpy as jnp
from jax import lax
from jax.sharding import PartitionSpec as P
from jax.experimental import pallas as pl
from jax.experimental.pallas import tpu as pltpu

SK = 128
MERGED_LEVELS = 4


half_inverse = 0.125
ridge_eps = 1e-05


def from_partner(value, axis, stride):
    mask = 2**stride
    pairs = [(source, source ^ mask) for source in range(lax.axis_size(axis))]
    return lax.ppermute(value, axis, pairs)


def split3(value):
    first = value.astype(jnp.bfloat16)
    rest = value - first.astype(jnp.float32)
    second = rest.astype(jnp.bfloat16)
    third = (rest - second.astype(jnp.float32)).astype(jnp.bfloat16)
    return first, second, third


def row_operand(leaf_points):
    norms = jnp.sum(leaf_points * leaf_points, axis=1)
    scaled = jnp.swapaxes(leaf_points, 1, 2) * (2.0 * half_inverse)
    place = lax.broadcasted_iota(jnp.int32, norms.shape + (8,), 2)
    tail = jnp.where(place == 0, -half_inverse, jnp.where(place == 1, -half_inverse * norms[:, :, None], 0.0))
    first, second, third = split3(jnp.concatenate([scaled, tail], axis=2))
    return jnp.concatenate([first, first, second, second, first, third], axis=2)


def sketch_kernel(slots_ref, counts_ref, row_ref, col_ref, code_ref, *refs):
    out_ref = refs[-1]
    leaves = out_ref.shape[0]
    points = col_ref.shape[2]
    place = lax.broadcasted_iota(jnp.int32, (8, points), 0)
    bucket_id = lax.broadcasted_iota(jnp.int32, (SK, points), 0)
    contract_last = (((1,), (1,)), ((), ()))
    for leaf in range(leaves):
        out_ref[leaf] = jnp.zeros(out_ref.shape[1:], jnp.float32)

        def tile(slot, carry):
            column = slots_ref[leaf, slot]
            y = col_ref[column]
            norms = jnp.sum(y * y, axis=0, keepdims=True)
            tail = jnp.where(place == 0, norms, jnp.where(place == 1, 1.0, 0.0))
            first, second, third = split3(jnp.concatenate([y, tail], axis=0))
            stacked = jnp.concatenate([first, second, first, second, third, first], axis=0)
            exponent = jnp.dot(row_ref[leaf], stacked, preferred_element_type=jnp.float32)
            kernel = jnp.exp(exponent)
            code = code_ref[pl.ds(column, 1), :]
            signs = (1 - 2 * (code // SK)).astype(jnp.float32)
            omega_t = jnp.where(bucket_id == code % SK, signs, 0.0).astype(jnp.bfloat16)
            high = kernel.astype(jnp.bfloat16)
            low = (kernel - high.astype(jnp.float32)).astype(jnp.bfloat16)
            terms = lax.dot_general(high, omega_t, contract_last, preferred_element_type=jnp.float32)
            terms = terms + lax.dot_general(low, omega_t, contract_last, preferred_element_type=jnp.float32)
            out_ref[leaf] += terms
            return carry

        def two_tiles(step, carry):
            return tile(2 * step + 1, tile(2 * step, carry))

        count = counts_ref[leaf]
        lax.fori_loop(0, count // 2, two_tiles, 0)
        lax.fori_loop((count // 2) * 2, count, tile, 0)


def accumulate(leaf_points, col_store, code_store, slot_table, pair_count, after=()):
    leaves, _, points = leaf_points.shape
    smem, vmem = pltpu.MemorySpace.SMEM, pltpu.MemorySpace.VMEM
    return pl.pallas_call(
        sketch_kernel,
        out_shape=jax.ShapeDtypeStruct((leaves, points, SK), jnp.float32),
        in_specs=[pl.BlockSpec(memory_space=smem)] * 2
        + [pl.BlockSpec(memory_space=vmem)] * 3
        + [pl.BlockSpec(memory_space=pl.ANY)] * len(after),
        out_specs=pl.BlockSpec(memory_space=vmem),
        compiler_params=pltpu.CompilerParams(vmem_limit_bytes=48 * 1024 * 1024),
        cost_estimate=pl.CostEstimate(
            flops=int(slot_table.size) * points * points * (96 + 4 * SK) * 2,
            transcendentals=int(slot_table.size) * points * points,
            bytes_accessed=int(slot_table.size) * points * 40 + leaves * points * SK * 4,
        ),
    )(slot_table, pair_count, row_operand(leaf_points), col_store, code_store, *after)


def cholesky_kernel(gram_ref, block_ref, total_ref, basis_ref, top_ref, out_ref):
    mats, rows, width = out_ref.shape
    leaves = gram_ref.shape[0]
    out_ref[:leaves, :width, :] = gram_ref[...]
    out_ref[:leaves, width:, :] = block_ref[...]
    out_ref[leaves:, :width, :] = total_ref[...]
    out_ref[leaves:, width:, :] = jnp.zeros((mats - leaves, rows - width, width), jnp.float32)
    for block in range(width // 8):
        low = block * 8
        shape = (rows - low, width)
        lane = lax.broadcasted_iota(jnp.int32, shape, 1)
        row = lax.broadcasted_iota(jnp.int32, shape, 0) + low
        parts = [out_ref[m, low:, :] for m in range(mats)]
        for t in range(8):
            j = low + t
            pick = lane == j
            later = lane > j
            for m in range(mats):
                a = parts[m]
                pivot_row = a[t : t + 1]
                pivot = jnp.sum(jnp.where(pick[:1], pivot_row, 0.0), axis=1, keepdims=True)
                scale = 1.0 / jnp.sqrt(pivot)
                column = jnp.sum(jnp.where(pick, a, 0.0), axis=1, keepdims=True) * scale
                column = jnp.where(row[:, :1] >= j, column, 0.0)
                updated = a - column * (pivot_row * scale)
                parts[m] = jnp.where(later, updated, jnp.where(pick, column, a))
        for m in range(mats):
            out_ref[m, low:, :] = parts[m]
    for m in range(leaves):
        basis_ref[m] = out_ref[m, width:, :]
    lane = lax.broadcasted_iota(jnp.int32, (width, width), 1)
    row = lax.broadcasted_iota(jnp.int32, (width, width), 0)
    for m in range(top_ref.shape[0]):
        top_ref[m] = jnp.where(row >= lane, out_ref[leaves + m, :width, :], 0.0).T


def cholesky_rows(gram, block, total):
    leaves, width, _ = gram.shape
    rows = width + block.shape[1]
    vmem = pltpu.MemorySpace.VMEM
    return pl.pallas_call(
        cholesky_kernel,
        out_shape=(
            jax.ShapeDtypeStruct(block.shape, jnp.float32),
            jax.ShapeDtypeStruct(total.shape, jnp.float32),
        ),
        in_specs=[pl.BlockSpec(memory_space=vmem)] * 3,
        out_specs=(pl.BlockSpec(memory_space=vmem), pl.BlockSpec(memory_space=vmem)),
        scratch_shapes=[pltpu.VMEM((leaves + total.shape[0], rows, width), jnp.float32)],
    )(gram, block, total)


def on_device(leaf_points, col_points, source_hash_signs, adjacent_leaf_lists, near_count):
    copies = jnp.broadcast_to(col_points, (lax.axis_size("row"),) + col_points.shape)
    owned = lax.all_to_all(copies, "row", 0, 0, tiled=True).reshape((1, -1) + col_points.shape[2:])
    leaves = leaf_points.shape[0]
    pair_count = near_count[:, 0]
    col_store = owned.reshape(owned.shape[1:])
    code_store = source_hash_signs.reshape(source_hash_signs.shape[1:])
    steps = lax.axis_size("col").bit_length() - 1
    per_leaf, taken = [], []

    def advance(e, upto):
        while taken[e] < min(upto, steps):
            per_leaf[e] = per_leaf[e] + from_partner(per_leaf[e], "col", taken[e])
            taken[e] += 1

    for leaf in range(leaves):
        for e in range(leaf):
            advance(e, leaf - 1 - e)
        after = tuple(per_leaf[e] for e in range(leaf) if taken[e] > 0)
        per_leaf.append(
            accumulate(
                leaf_points[leaf : leaf + 1],
                col_store,
                code_store,
                adjacent_leaf_lists[leaf : leaf + 1],
                pair_count[leaf : leaf + 1],
                after,
            )
        )
        taken.append(0)
    for e in range(leaves):
        advance(e, steps)
    samples = jnp.concatenate(per_leaf, axis=0)
    rows = samples.shape[1] // lax.axis_size("col")
    rows_part = lax.dynamic_slice_in_dim(samples, lax.axis_index("col") * rows, rows, axis=1)
    gram = jnp.einsum("bri,brk->bik", samples, samples, precision=lax.Precision.HIGHEST)
    ridge = jnp.trace(gram, axis1=1, axis2=2) / SK + ridge_eps
    shifted = gram + ridge[:, None, None] * jnp.eye(SK, dtype=jnp.float32)[None]
    total = jnp.sum(shifted, axis=0)
    local_levels = leaves.bit_length() - 1
    for bit in range(MERGED_LEVELS - local_levels):
        total = total + from_partner(total, "row", bit)
    leaf_basis, factor = cholesky_rows(shifted, rows_part, total[None])
    return (leaf_basis, factor)


def solution(mesh):
    return jax.shard_map(
        on_device,
        mesh=mesh,
        in_specs=(
            P("row", None, None),
            P("col", "row", None, None),
            P("col", None, None),
            P("row", "col"),
            P("row", "col"),
        ),
        out_specs=(P("row", "col", None), P("row", None, None)),
        check_vma=False,
    )
```

```python
from functools import partial

import jax
import jax.numpy as jnp
from jax import lax
from jax.sharding import PartitionSpec as P
from jax.experimental import pallas as pl
from jax.experimental.pallas import tpu as pltpu

SK = 128
MERGED_LEVELS = 4


half_inverse = 0.125
ridge_eps = 1e-05


def from_partner(value, axis, stride):
    mask = 2**stride
    pairs = [(source, source ^ mask) for source in range(lax.axis_size(axis))]
    return lax.ppermute(value, axis, pairs)


def split3(value):
    first = value.astype(jnp.bfloat16)
    rest = value - first.astype(jnp.float32)
    second = rest.astype(jnp.bfloat16)
    third = (rest - second.astype(jnp.float32)).astype(jnp.bfloat16)
    return first, second, third


def row_operand(leaf_points):
    norms = jnp.sum(leaf_points * leaf_points, axis=1)
    scaled = jnp.swapaxes(leaf_points, 1, 2) * (2.0 * half_inverse)
    place = lax.broadcasted_iota(jnp.int32, norms.shape + (8,), 2)
    tail = jnp.where(place == 0, -half_inverse, jnp.where(place == 1, -half_inverse * norms[:, :, None], 0.0))
    first, second, third = split3(jnp.concatenate([scaled, tail], axis=2))
    return jnp.concatenate([first, first, second, second, first, third], axis=2)


def sketch_kernel(slots_ref, counts_ref, row_ref, col_ref, code_ref, *refs):
    out_ref = refs[-1]
    leaves = out_ref.shape[0]
    points = col_ref.shape[2]
    place = lax.broadcasted_iota(jnp.int32, (8, points), 0)
    bucket_id = lax.broadcasted_iota(jnp.int32, (SK, points), 0)
    contract_last = (((1,), (1,)), ((), ()))
    for leaf in range(leaves):
        out_ref[leaf] = jnp.zeros(out_ref.shape[1:], jnp.float32)

        def tile(slot, carry):
            column = slots_ref[leaf, slot]
            y = col_ref[column]
            norms = jnp.sum(y * y, axis=0, keepdims=True)
            tail = jnp.where(place == 0, norms, jnp.where(place == 1, 1.0, 0.0))
            first, second, third = split3(jnp.concatenate([y, tail], axis=0))
            stacked = jnp.concatenate([first, second, first, second, third, first], axis=0)
            exponent = jnp.dot(row_ref[leaf], stacked, preferred_element_type=jnp.float32)
            kernel = jnp.exp(exponent)
            code = code_ref[pl.ds(column, 1), :]
            signs = (1 - 2 * (code // SK)).astype(jnp.float32)
            omega_t = jnp.where(bucket_id == code % SK, signs, 0.0).astype(jnp.bfloat16)
            high = kernel.astype(jnp.bfloat16)
            low = (kernel - high.astype(jnp.float32)).astype(jnp.bfloat16)
            terms = lax.dot_general(high, omega_t, contract_last, preferred_element_type=jnp.float32)
            terms = terms + lax.dot_general(low, omega_t, contract_last, preferred_element_type=jnp.float32)
            out_ref[leaf] += terms
            return carry

        def four_tiles(step, carry):
            for k in range(4):
                carry = tile(4 * step + k, carry)
            return carry

        count = counts_ref[leaf]
        lax.fori_loop(0, count // 4, four_tiles, 0)
        lax.fori_loop((count // 4) * 4, count, tile, 0)


def accumulate(leaf_points, col_store, code_store, slot_table, pair_count, after=()):
    leaves, _, points = leaf_points.shape
    smem, vmem = pltpu.MemorySpace.SMEM, pltpu.MemorySpace.VMEM
    return pl.pallas_call(
        sketch_kernel,
        out_shape=jax.ShapeDtypeStruct((leaves, points, SK), jnp.float32),
        in_specs=[pl.BlockSpec(memory_space=smem)] * 2
        + [pl.BlockSpec(memory_space=vmem)] * 3
        + [pl.BlockSpec(memory_space=pl.ANY)] * len(after),
        out_specs=pl.BlockSpec(memory_space=vmem),
        compiler_params=pltpu.CompilerParams(vmem_limit_bytes=48 * 1024 * 1024),
        cost_estimate=pl.CostEstimate(
            flops=int(slot_table.size) * points * points * (96 + 4 * SK) * 2,
            transcendentals=int(slot_table.size) * points * points,
            bytes_accessed=int(slot_table.size) * points * 40 + leaves * points * SK * 4,
        ),
    )(slot_table, pair_count, row_operand(leaf_points), col_store, code_store, *after)


def cholesky_kernel(in_ref, basis_ref, top_ref, out_ref):
    mats, rows, width = in_ref.shape
    out_ref[...] = in_ref[...]
    for block in range(width // 8):
        low = block * 8
        shape = (rows - low, width)
        lane = lax.broadcasted_iota(jnp.int32, shape, 1)
        row = lax.broadcasted_iota(jnp.int32, shape, 0) + low
        parts = [out_ref[m, low:, :] for m in range(mats)]
        for t in range(8):
            j = low + t
            pick = lane == j
            later = lane > j
            for m in range(mats):
                a = parts[m]
                pivot_row = a[t : t + 1]
                pivot = jnp.sum(jnp.where(pick[:1], pivot_row, 0.0), axis=1, keepdims=True)
                scale = 1.0 / jnp.sqrt(pivot)
                column = jnp.sum(jnp.where(pick, a, 0.0), axis=1, keepdims=True) * scale
                column = jnp.where(row[:, :1] >= j, column, 0.0)
                updated = a - column * (pivot_row * scale)
                parts[m] = jnp.where(later, updated, jnp.where(pick, column, a))
        for m in range(mats):
            out_ref[m, low:, :] = parts[m]
    leaves = basis_ref.shape[0]
    for m in range(leaves):
        basis_ref[m] = out_ref[m, width:, :]
    lane = lax.broadcasted_iota(jnp.int32, (width, width), 1)
    row = lax.broadcasted_iota(jnp.int32, (width, width), 0)
    for m in range(top_ref.shape[0]):
        top_ref[m] = jnp.where(row >= lane, out_ref[leaves + m, :width, :], 0.0).T


def cholesky_rows(stacked, leaves):
    mats, rows, width = stacked.shape
    vmem = pltpu.MemorySpace.VMEM
    return pl.pallas_call(
        cholesky_kernel,
        out_shape=(
            jax.ShapeDtypeStruct((leaves, rows - width, width), jnp.float32),
            jax.ShapeDtypeStruct((mats - leaves, width, width), jnp.float32),
        ),
        in_specs=[pl.BlockSpec(memory_space=vmem)],
        out_specs=(pl.BlockSpec(memory_space=vmem), pl.BlockSpec(memory_space=vmem)),
        scratch_shapes=[pltpu.VMEM(stacked.shape, jnp.float32)],
    )(stacked)


def on_device(leaf_points, col_points, source_hash_signs, adjacent_leaf_lists, near_count):
    copies = jnp.broadcast_to(col_points, (lax.axis_size("row"),) + col_points.shape)
    owned = lax.all_to_all(copies, "row", 0, 0, tiled=True).reshape((1, -1) + col_points.shape[2:])
    leaves = leaf_points.shape[0]
    pair_count = near_count[:, 0]
    col_store = owned.reshape(owned.shape[1:])
    code_store = source_hash_signs.reshape(source_hash_signs.shape[1:])
    steps = lax.axis_size("col").bit_length() - 1
    per_leaf, taken = [], []

    def advance(e, upto):
        while taken[e] < min(upto, steps):
            per_leaf[e] = per_leaf[e] + from_partner(per_leaf[e], "col", taken[e])
            taken[e] += 1

    for leaf in range(leaves):
        for e in range(leaf):
            advance(e, leaf - 1 - e)
        after = tuple(per_leaf[e] for e in range(leaf) if taken[e] > 0)
        per_leaf.append(
            accumulate(
                leaf_points[leaf : leaf + 1],
                col_store,
                code_store,
                adjacent_leaf_lists[leaf : leaf + 1],
                pair_count[leaf : leaf + 1],
                after,
            )
        )
        taken.append(0)
    for e in range(leaves):
        advance(e, steps)
    samples = jnp.concatenate(per_leaf, axis=0)
    rows = samples.shape[1] // lax.axis_size("col")
    rows_part = lax.dynamic_slice_in_dim(samples, lax.axis_index("col") * rows, rows, axis=1)
    gram = jnp.einsum("bri,brk->bik", samples, samples, precision=lax.Precision.HIGHEST)
    ridge = jnp.trace(gram, axis1=1, axis2=2) / SK + ridge_eps
    shifted = gram + ridge[:, None, None] * jnp.eye(SK, dtype=jnp.float32)[None]
    total = jnp.sum(shifted, axis=0)
    local_levels = leaves.bit_length() - 1
    for bit in range(MERGED_LEVELS - local_levels):
        total = total + from_partner(total, "row", bit)
    stacked = jnp.concatenate(
        [
            jnp.concatenate([shifted, rows_part], axis=1),
            jnp.concatenate([total, jnp.zeros_like(rows_part[0])], axis=0)[None],
        ],
        axis=0,
    )
    leaf_basis, factor = cholesky_rows(stacked, leaves)
    return (leaf_basis, factor)


def solution(mesh):
    return jax.shard_map(
        on_device,
        mesh=mesh,
        in_specs=(
            P("row", None, None),
            P("col", "row", None, None),
            P("col", None, None),
            P("row", "col"),
            P("row", "col"),
        ),
        out_specs=(P("row", "col", None), P("row", None, None)),
        check_vma=False,
    )
```
